256 devices in a mesh: tm: 32 (over z, y), expert: 8 (over x, core).
Axes of the slice: x: 4, y: 4, z: 8, core: 2. Of those that a mesh axis runs over, the one named last changes fastest.
Arguments:
- frames: bfloat16 [8, 8192, 1024], P('expert', 'tm'), may hold values from -6 to 6
- utt_lengths: int32 [8, 32], P('expert'), may hold values from 1 to 512, 8192 in all within a row
- expert_ids: int32 [8, 8192, 1], P('expert', 'tm'), may hold values from 0 to 63; in each aligned block of 256 rows (0 to 255, 256 to 511, ..., all dimensions but the last counted through in order) at most 8 rows name the same one
- point_in: bfloat16 [1024, 2048], replicated, may hold values from -0.1875 to 0.1875
- depth_taps: float32 [31, 1024], replicated, may hold values from -1 to 1
- norm_scale: float32 [1024], replicated, may hold values from 0.5 to 2
- norm_shift: float32 [1024], replicated, may hold values from -3 to 3
- point_out: bfloat16 [1024, 1024], replicated, may hold values from -0.1875 to 0.1875
- router: bfloat16 [1024, 64], replicated, may hold values from -0.1875 to 0.1875
- expert_in: bfloat16 [8, 32, 1024, 1024], P('expert', 'tm'), may hold values from -0.1875 to 0.1875
- expert_out: bfloat16 [8, 32, 1024, 1024], P('expert', 'tm'), may hold values from -0.09375 to 0.09375
Outputs:
- layer_out: bfloat16 [8, 8192, 1024], P('expert', 'tm')
The draws below stay inside these ranges and needn't reach their ends.
Inputs may be any that keep to these rules, and one draw needn't show every extreme that they name: `expert_ids`: in the 256 frames of one device (aligned blocks of a stream) no expert is named more than 8 times; in some such blocks one expert is named exactly 8 times. `utt_lengths`: the lengths of each stream sum to 8192; the longest is exactly 512.
All inputs are finite; a program needn't handle non-finite values.
Results may differ from the reference program's by a relative error of at most 0.006.
Values may be sent and summed in bfloat16 or wider, within the bound.
No kernel may reach another device: no remote copies, remote signals or barrier semaphores. Data moves between devices by JAX's collectives and lax.ppermute only.
A program may use at most 64 MiB of HBM per device.

```python
import math
import jax
import jax.numpy as jnp
import numpy as np
from jax import lax

D = 1024
FF = 4096
KERNEL = 31
QUARTERS = 4
TOK_DEV = 256
STREAMS = 8
STREAM_LEN = 8192
UTTS = 32
LMAX = 512
EXPERTS = 64
EXP_GROUPS = 8
SLICES = 32
FF_DEV = 1024
CAP = 8


def block_scale(own_key, shape, split, low, largest):
    factor_of, own = 1.0, jax.random.fold_in(own_key, 6)
    for dim, blocks in split:
        draws = jnp.exp(jax.random.uniform(jax.random.fold_in(own, dim), (blocks,), jnp.float32, low / len(split), largest / len(split)))
        factor_of = factor_of * jnp.repeat(draws, shape[dim] // blocks).reshape([-1 if axis == dim else 1 for axis in range(len(shape))])
    return factor_of


def split_up(number_of, total, limit, slope):
    portions = [(1 << 20) // math.isqrt(grade ** slope) + 1 for grade in range(2, number_of + 1)]
    surplus, holding = total - limit - (number_of - 1), [1] * (number_of - 1)
    while surplus > 0:
        free = [i for i in range(number_of - 1) if holding[i] < limit]
        mass, budget = sum([portions[i] for i in free]), surplus
        for i in free:
            addition = min(limit - holding[i], max(1, budget * portions[i] // mass), surplus)
            holding[i] = holding[i] + addition
            surplus = surplus - addition
    return np.array([limit] + holding)


def uneven_parts(own_key, amount, total, bound, lean):
    if amount == 2:
        one = jax.random.randint(own_key, (), max(1, total - bound), min(bound, total - 1) + 1)
        return jnp.stack([one, total - one])
    sizes = jnp.asarray(split_up(amount, total, bound, lean), jnp.int32)
    twos = (amount - 1) // 2
    giver, taker = sizes[1:1 + 2 * twos:2], sizes[2:2 + 2 * twos:2]
    margin = jnp.minimum(giver - 1, bound - taker)
    shifted = jax.random.randint(jax.random.fold_in(own_key, 1), (twos,), 0, 1 << 20) % (margin + 1)
    sizes = sizes.at[1:1 + 2 * twos:2].set(giver - shifted).at[2:2 + 2 * twos:2].set(taker + shifted)
    return sizes[jax.random.permutation(jax.random.fold_in(own_key, 2), amount)]


def assign_block(rng, own, number, rows, number_of, top, bound, skew):
    ranking = jax.random.permutation(rng, number_of)
    heavy_load, common = portions_of(number_of, rows * top, bound, skew, True), portions_of(number_of, rows * top, bound, skew, False)
    places = jnp.arange(number_of)

    def named(sizes, offset_by):
        used = int((sizes > 0).sum())
        fixed = max(1, used // 4)
        moved = fixed + (places - fixed + offset_by * (used - fixed)) % max(1, number_of - fixed)
        return jnp.zeros((number_of,), jnp.int32).at[ranking[jnp.where(places < fixed, places, moved)]].set(jnp.asarray(sizes, jnp.int32))

    sizes = jnp.where(number % 4 == 0, named(heavy_load, number // 4), named(common, number - number // 4 - 1))
    mixed = jax.random.permutation(jax.random.fold_in(own, 3), number_of)
    source_of, receiver = mixed[0:number_of // 2 * 2:2], mixed[1:number_of // 2 * 2:2]
    slack = jnp.minimum(sizes[source_of] - 1, bound - sizes[receiver]) // 2
    slack = jnp.where((source_of == ranking[0]) | (receiver == ranking[0]) | (sizes[receiver] == 0), 0, jnp.maximum(slack, 0))
    moved = jax.random.randint(jax.random.fold_in(own, 4), (number_of // 2,), 0, 1 << 20) % (slack + 1)
    sizes = sizes.at[source_of].add(-moved).at[receiver].add(moved)
    members = jnp.searchsorted(jnp.cumsum(sizes), jnp.arange(rows * top), side="right").astype(jnp.int32)
    grid = members.reshape(top, rows).T
    grid = grid[jax.random.permutation(jax.random.fold_in(own, 1), rows)]
    offset_by = jax.random.randint(jax.random.fold_in(own, 2), (rows, 1), 0, top)
    return jnp.take_along_axis(grid, (jnp.arange(top)[None, :] + offset_by) % top, axis=1)


def portions_of(count, total, limit, slope, full):
    portions = [(1 << 20) // math.isqrt(rank ** slope) + 1 for rank in range(1, count + 1)]
    largest = limit if full else min(limit, max(-(-total // count), total * portions[0] // sum(portions)))
    least = 1 if total - largest >= count - 1 else 0
    counts, surplus = [largest] + [least] * (count - 1), total - largest - least * (count - 1)
    while surplus > 0:
        movable = [i for i in range(1, count) if counts[i] < largest] or [i for i in range(1, count) if counts[i] < limit]
        pool, left = sum([portions[i] for i in movable]), surplus
        for i in movable:
            more = min(limit - counts[i], max(1, left * portions[i] // pool), surplus)
            counts[i] = counts[i] + more
            surplus = surplus - more
    return np.array(counts)


def bell_draw(rng, dims, deviation, reach, pieces=(), kind=jnp.bfloat16):
    result = jax.random.normal(rng, dims, jnp.float32) * deviation
    if len(pieces) > 0:
        result = block_scale(rng, dims, pieces, -0.22, 0.18) * result
    return jnp.clip(result, min=-reach, max=reach).astype(kind)


def setup_inputs(seed: int = 0) -> dict:
    key_of = jax.random.split(jax.random.key(seed), 12)
    frames = bell_draw(key_of[0], (STREAMS, STREAM_LEN, D), 1.0, 6.0, ((0, 8), (1, 32)))
    utt_lengths = jax.vmap(lambda own: uneven_parts(own, UTTS, STREAM_LEN, LMAX, 2))(jax.random.split(key_of[1], STREAMS)).reshape((STREAMS, UTTS)).astype(jnp.int32)
    expert_ids_keys = jax.random.split(jax.random.fold_in(key_of[2], 1), STREAMS * STREAM_LEN // TOK_DEV)
    expert_ids_turns = jax.random.permutation(jax.random.fold_in(key_of[2], 3), STREAMS * STREAM_LEN // TOK_DEV)
    expert_ids = jax.vmap(lambda own, number: assign_block(jax.random.fold_in(key_of[2], 2), own, number, TOK_DEV, EXPERTS, 1, CAP, 2))(expert_ids_keys, expert_ids_turns).reshape((STREAMS, STREAM_LEN, 1))
    point_in = bell_draw(key_of[3], (D, 2 * D), D ** -0.5, 0.1875)
    depth_taps = bell_draw(key_of[4], (KERNEL, D), KERNEL ** -0.5, 1.0, (), jnp.float32)
    norm_scale = jnp.clip(jnp.exp(jax.random.uniform(key_of[5], (D,), jnp.float32, math.log(0.5), math.log(2.0))), 0.5, 2.0)
    norm_shift = bell_draw(key_of[6], (D,), 0.5, 3.0, (), jnp.float32)
    point_out = bell_draw(key_of[7], (D, D), D ** -0.5, 0.1875)
    router = bell_draw(key_of[8], (D, EXPERTS), D ** -0.5, 0.1875)
    expert_in = bell_draw(key_of[9], (EXP_GROUPS, SLICES, D, FF_DEV), D ** -0.5, 0.1875, ((0, 8), (1, 32)))
    expert_out = bell_draw(key_of[10], (EXP_GROUPS, SLICES, FF_DEV, D), FF ** -0.5, 0.09375, ((0, 8), (1, 32)))
    return {"frames": frames, "utt_lengths": utt_lengths, "expert_ids": expert_ids, "point_in": point_in, "depth_taps": depth_taps, "norm_scale": norm_scale, "norm_shift": norm_shift, "point_out": point_out, "router": router, "expert_in": expert_in, "expert_out": expert_out}


def layer_norm(values):
    values = values.astype(jnp.float32)
    center = values - lax.optimization_barrier(jnp.mean(values, axis=-1, keepdims=True))
    variance = lax.optimization_barrier(jnp.mean(center * center, axis=-1, keepdims=True))
    return center * lax.rsqrt(variance + 1e-05)

def conv_stream(signal, lengths, point_in, depth_taps, norm_scale, norm_shift, point_out):
    frame_count = signal.shape[0]
    half_span = (KERNEL - 1) // 2
    normed = layer_norm(signal).astype(jnp.bfloat16)
    projected = jnp.dot(normed, point_in, preferred_element_type=jnp.float32)
    gated_act = (projected[:, :D] * jax.nn.sigmoid(projected[:, D:])).astype(jnp.bfloat16)
    utter_ends = jnp.cumsum(lengths, dtype=jnp.int32)
    utter_starts = utter_ends - lengths
    position = jnp.arange(frame_count, dtype=jnp.int32)
    inside = (utter_starts[None, :] <= position[:, None]) & (position[:, None] < utter_ends[None, :])
    first_pos = lax.optimization_barrier(jnp.sum(jnp.where(inside, utter_starts[None, :], 0), axis=1, dtype=jnp.int32))
    last_pos = lax.optimization_barrier(jnp.sum(jnp.where(inside, utter_ends[None, :], 0), axis=1, dtype=jnp.int32))
    padded = jnp.pad(gated_act, ((half_span, half_span), (0, 0)))
    depth_sum = jnp.zeros((frame_count, D), jnp.float32)
    for tap_index in range(KERNEL):
        nearby = position + (tap_index - half_span)
        inside_tap = ((nearby >= first_pos) & (nearby < last_pos)).astype(jnp.float32)
        window = padded[tap_index:tap_index + frame_count].astype(jnp.float32)
        depth_sum = depth_sum + depth_taps[tap_index][None, :] * window * inside_tap[:, None]
    activated = jax.nn.silu(depth_sum * norm_scale[None, :] + norm_shift[None, :]).astype(jnp.bfloat16)
    mixed_res = signal.astype(jnp.float32) + jnp.dot(activated, point_out, preferred_element_type=jnp.float32)
    return mixed_res.astype(jnp.bfloat16)

def run_expert(packed):
    slot_rows, w_in_all, w_out_all = packed
    total_sum = jnp.zeros(slot_rows.shape, jnp.float32)
    for quarter in range(QUARTERS):
        hidden = jax.nn.silu(jnp.dot(slot_rows, w_in_all[quarter], preferred_element_type=jnp.float32)).astype(jnp.bfloat16)
        partial_out = jnp.dot(hidden, w_out_all[quarter], preferred_element_type=jnp.float32).astype(jnp.bfloat16)
        total_sum = total_sum + partial_out.astype(jnp.float32)
    return total_sum.astype(jnp.bfloat16)

def reference(frames, utt_lengths, expert_ids, point_in, depth_taps, norm_scale, norm_shift, point_out, router, expert_in, expert_out):
    mixed_list = []
    for stream_index in range(STREAMS):
        mixed_list.append(conv_stream(frames[stream_index], utt_lengths[stream_index], point_in, depth_taps, norm_scale, norm_shift, point_out))
    mixed_res = jnp.stack(mixed_list)
    flat_mixed = mixed_res.reshape(-1, D)
    flat_in = layer_norm(flat_mixed).astype(jnp.bfloat16)
    flat_route = expert_ids.reshape(-1).astype(jnp.int32)
    logits = jnp.dot(flat_in, router, preferred_element_type=jnp.float32)
    gate_value = jax.nn.sigmoid(jnp.take_along_axis(logits, flat_route[:, None], axis=1)[:, 0])
    sources = flat_route.shape[0] // TOK_DEV
    blocks = flat_route.reshape(sources, TOK_DEV)
    labels = jnp.arange(EXPERTS, dtype=jnp.int32)
    onehot = (blocks[:, :, None] == labels[None, None, :]).astype(jnp.int32)
    earlier = jnp.cumsum(onehot, axis=1, dtype=jnp.int32) - onehot
    rank_in = lax.optimization_barrier(jnp.sum(earlier * onehot, axis=2, dtype=jnp.int32))
    slot_flat = (jnp.arange(sources, dtype=jnp.int32)[:, None] * CAP + rank_in).reshape(-1).astype(jnp.int32)
    buffers = jnp.zeros((EXPERTS, sources * CAP, D), jnp.bfloat16).at[flat_route, slot_flat].set(flat_in)
    weights_in = expert_in.reshape(EXPERTS, QUARTERS, D, FF_DEV)
    weights_out = expert_out.reshape(EXPERTS, QUARTERS, FF_DEV, D)
    results = lax.map(run_expert, (buffers, weights_in, weights_out))
    frame_moe = results[flat_route, slot_flat]
    layer_out = flat_mixed.astype(jnp.float32) + gate_value[:, None] * frame_moe.astype(jnp.float32)
    return layer_out.astype(jnp.bfloat16).reshape(STREAMS, STREAM_LEN, D)
```

```python
import jax
import jax.numpy as jnp
from jax import lax
from jax.sharding import Mesh, PartitionSpec as P

QUARTERS = 4


def padded_2(cells, sides, width):
    for axis, dim in sides:
        count = lax.axis_size(axis)
        ends = count - 1
        head = lax.slice_in_dim(cells, 0, width, axis=dim)
        tail = lax.slice_in_dim(cells, cells.shape[dim] - width, cells.shape[dim], axis=dim)
        cells = jnp.concatenate(
            [
                lax.ppermute(tail, axis, [(i, (i + 1) % count) for i in range(ends)]),
                cells,
                lax.ppermute(head, axis, [((i + 1) % count, i) for i in range(ends)]),
            ],
            axis=dim,
        )
    return cells


def layer_norm(values):
    values = values.astype(jnp.float32)
    center = values - jnp.mean(values, axis=-1, keepdims=True)
    variance = jnp.mean(center * center, axis=-1, keepdims=True)
    return center * lax.rsqrt(variance + 1e-05)


def expert_pass(slot_block, w_in, w_out):
    slot_rows = slot_block.reshape(-1, slot_block.shape[-1])
    hidden = jax.nn.silu(jnp.dot(slot_rows, w_in, preferred_element_type=jnp.float32)).astype(
        jnp.bfloat16
    )
    partial_out = jnp.dot(hidden, w_out, preferred_element_type=jnp.float32).astype(jnp.bfloat16)
    return partial_out.reshape(slot_block.shape)


def shards(
    frames,
    utt_lengths,
    expert_ids,
    point_in,
    depth_taps,
    norm_scale,
    norm_shift,
    point_out,
    router,
    expert_in,
    expert_out,
):
    signal = frames[0]
    frame_count, model_width = signal.shape
    tap_count = depth_taps.shape[0]
    half_span = (tap_count - 1) // 2
    normed = layer_norm(signal).astype(jnp.bfloat16)
    projected = jnp.dot(normed, point_in, preferred_element_type=jnp.float32)
    gated_act = (projected[:, :model_width] * jax.nn.sigmoid(projected[:, model_width:])).astype(
        jnp.bfloat16
    )
    padded = padded_2(gated_act, ((("z", "y"), 0),), half_span)
    lengths = utt_lengths[0]
    utter_ends = jnp.cumsum(lengths, dtype=jnp.int32)
    utter_starts = utter_ends - lengths
    position = (lax.axis_index("z") * lax.axis_size("y") + lax.axis_index("y")) * frame_count + jnp.arange(frame_count, dtype=jnp.int32)
    inside = (utter_starts[None, :] <= position[:, None]) & (
        position[:, None] < utter_ends[None, :]
    )
    first_pos = jnp.sum(jnp.where(inside, utter_starts[None, :], 0), axis=1, dtype=jnp.int32)
    last_pos = jnp.sum(jnp.where(inside, utter_ends[None, :], 0), axis=1, dtype=jnp.int32)
    depth_sum = jnp.zeros((frame_count, model_width), jnp.float32)
    for tap_index in range(tap_count):
        nearby = position + (tap_index - half_span)
        inside_tap = ((nearby >= first_pos) & (nearby < last_pos)).astype(jnp.float32)
        window = padded[tap_index : tap_index + frame_count].astype(jnp.float32)
        depth_sum = depth_sum + depth_taps[tap_index][None, :] * window * inside_tap[:, None]
    activated = jax.nn.silu(depth_sum * norm_scale[None, :] + norm_shift[None, :]).astype(
        jnp.bfloat16
    )
    mixed_res = (
        signal.astype(jnp.float32)
        + jnp.dot(activated, point_out, preferred_element_type=jnp.float32)
    ).astype(jnp.bfloat16)
    moe_in = layer_norm(mixed_res).astype(jnp.bfloat16)
    route_ids = expert_ids[0, :, 0]
    expert_count = router.shape[1]
    capacity = 2 * frame_count // expert_count
    owners = lax.axis_size("expert")
    per_owner = expert_count // owners
    labels = jnp.arange(expert_count, dtype=jnp.int32)
    onehot = (route_ids[:, None] == labels[None, :]).astype(jnp.int32)
    earlier = jnp.cumsum(onehot, axis=0, dtype=jnp.int32) - onehot
    rank_in = jnp.sum(earlier * onehot, axis=1, dtype=jnp.int32)
    logits = jnp.dot(moe_in, router, preferred_element_type=jnp.float32)
    gate_value = jax.nn.sigmoid(jnp.sum(logits * onehot.astype(jnp.float32), axis=1))
    owner_group = route_ids // per_owner
    member = route_ids % per_owner
    slot_index = (member * owners + owner_group) * capacity + rank_in
    send_buffer = (
        jnp.zeros((per_owner * owners * capacity, model_width), jnp.bfloat16)
        .at[slot_index]
        .set(moe_in)
    )
    send_buffer = send_buffer.reshape(per_owner, owners, capacity, model_width)
    w_in = expert_in[0, 0]
    w_out = expert_out[0, 0]
    by_group = lax.all_to_all(send_buffer, "expert", split_axis=1, concat_axis=1, tiled=True)
    by_member = lax.all_to_all(by_group, "z", split_axis=0, concat_axis=0, tiled=True)
    gathered = lax.all_gather(by_member, "y", axis=0, tiled=False)
    partial_out = expert_pass(gathered, w_in, w_out)
    returned = lax.all_to_all(partial_out, "y", split_axis=0, concat_axis=0, tiled=False)
    summed = jnp.sum(returned.astype(jnp.float32), axis=0).astype(jnp.bfloat16)
    results = lax.all_to_all(summed, "z", split_axis=0, concat_axis=0, tiled=True)
    results = lax.all_to_all(results, "expert", split_axis=1, concat_axis=1, tiled=True)
    frame_moe = results.reshape(-1, model_width)[slot_index]
    layer_out = mixed_res.astype(jnp.float32) + gate_value[:, None] * frame_moe.astype(jnp.float32)
    return layer_out.astype(jnp.bfloat16)[None]


def solution(mesh):
    tm_size = mesh.shape["tm"]
    y_size = QUARTERS
    split_mesh = Mesh(
        mesh.devices.reshape(tm_size // y_size, y_size, mesh.shape["expert"]), ("z", "y", "expert")
    )
    frames_spec = P("expert", ("z", "y"), None)
    weights_spec = P("expert", ("z", "y"), None, None)
    return jax.shard_map(
        shards,
        mesh=split_mesh,
        in_specs=(
            frames_spec,
            P("expert", None),
            frames_spec,
            P(),
            P(),
            P(),
            P(),
            P(),
            P(),
            weights_spec,
            weights_spec,
        ),
        out_specs=frames_spec,
        check_vma=False,
    )
```

```python
import jax
import jax.numpy as jnp
from jax import lax
from jax.sharding import Mesh, PartitionSpec as P

QUARTERS = 4


def padded_2(cells, sides, width):
    for axis, dim in sides:
        count = lax.axis_size(axis)
        ends = count - 1
        head = lax.slice_in_dim(cells, 0, width, axis=dim)
        tail = lax.slice_in_dim(cells, cells.shape[dim] - width, cells.shape[dim], axis=dim)
        cells = jnp.concatenate(
            [
                lax.ppermute(tail, axis, [(i, (i + 1) % count) for i in range(ends)]),
                cells,
                lax.ppermute(head, axis, [((i + 1) % count, i) for i in range(ends)]),
            ],
            axis=dim,
        )
    return cells


def shifted_exchange(blocks, axis, dim, back=False):
    count = lax.axis_size(axis)
    pieces = []
    for shift in range(count):
        piece = lax.index_in_dim(blocks, shift, axis=dim, keepdims=True)
        if shift:
            step = -shift if back else shift
            piece = lax.ppermute(piece, axis, [(i, (i + step) % count) for i in range(count)])
        pieces.append(piece)
    return jnp.concatenate(pieces, axis=dim)


def layer_norm(values):
    values = values.astype(jnp.float32)
    center = values - jnp.mean(values, axis=-1, keepdims=True)
    variance = jnp.mean(center * center, axis=-1, keepdims=True)
    return center * lax.rsqrt(variance + 1e-05)


def expert_pass(slot_block, w_in, w_out):
    slot_rows = slot_block.reshape(-1, slot_block.shape[-1])
    hidden = jax.nn.silu(jnp.dot(slot_rows, w_in, preferred_element_type=jnp.float32)).astype(
        jnp.bfloat16
    )
    partial_out = jnp.dot(hidden, w_out, preferred_element_type=jnp.float32).astype(jnp.bfloat16)
    return partial_out.reshape(slot_block.shape)


def shards(
    frames,
    utt_lengths,
    expert_ids,
    point_in,
    depth_taps,
    norm_scale,
    norm_shift,
    point_out,
    router,
    expert_in,
    expert_out,
):
    signal = frames[0]
    frame_count, model_width = signal.shape
    tap_count = depth_taps.shape[0]
    half_span = (tap_count - 1) // 2
    normed = layer_norm(signal).astype(jnp.bfloat16)
    projected = jnp.dot(normed, point_in, preferred_element_type=jnp.float32)
    gated_act = (projected[:, :model_width] * jax.nn.sigmoid(projected[:, model_width:])).astype(
        jnp.bfloat16
    )
    padded = padded_2(gated_act, ((("z", "y"), 0),), half_span)
    lengths = utt_lengths[0]
    utter_ends = jnp.cumsum(lengths, dtype=jnp.int32)
    utter_starts = utter_ends - lengths
    position = (lax.axis_index("z") * lax.axis_size("y") + lax.axis_index("y")) * frame_count + jnp.arange(frame_count, dtype=jnp.int32)
    inside = (utter_starts[None, :] <= position[:, None]) & (
        position[:, None] < utter_ends[None, :]
    )
    first_pos = jnp.sum(jnp.where(inside, utter_starts[None, :], 0), axis=1, dtype=jnp.int32)
    last_pos = jnp.sum(jnp.where(inside, utter_ends[None, :], 0), axis=1, dtype=jnp.int32)
    depth_sum = jnp.zeros((frame_count, model_width), jnp.float32)
    for tap_index in range(tap_count):
        nearby = position + (tap_index - half_span)
        inside_tap = ((nearby >= first_pos) & (nearby < last_pos)).astype(jnp.float32)
        window = padded[tap_index : tap_index + frame_count].astype(jnp.float32)
        depth_sum = depth_sum + depth_taps[tap_index][None, :] * window * inside_tap[:, None]
    activated = jax.nn.silu(depth_sum * norm_scale[None, :] + norm_shift[None, :]).astype(
        jnp.bfloat16
    )
    mixed_res = (
        signal.astype(jnp.float32)
        + jnp.dot(activated, point_out, preferred_element_type=jnp.float32)
    ).astype(jnp.bfloat16)
    moe_in = layer_norm(mixed_res).astype(jnp.bfloat16)
    route_ids = expert_ids[0, :, 0]
    expert_count = router.shape[1]
    capacity = 2 * frame_count // expert_count
    owners = lax.axis_size("expert")
    per_owner = expert_count // owners
    labels = jnp.arange(expert_count, dtype=jnp.int32)
    onehot = (route_ids[:, None] == labels[None, :]).astype(jnp.int32)
    earlier = jnp.cumsum(onehot, axis=0, dtype=jnp.int32) - onehot
    rank_in = jnp.sum(earlier * onehot, axis=1, dtype=jnp.int32)
    logits = jnp.dot(moe_in, router, preferred_element_type=jnp.float32)
    gate_value = jax.nn.sigmoid(jnp.sum(logits * onehot.astype(jnp.float32), axis=1))
    owner_group = (route_ids // per_owner - lax.axis_index("expert")) % owners
    member = (route_ids % per_owner - lax.axis_index("z")) % per_owner
    slot_index = (member * owners + owner_group) * capacity + rank_in
    send_buffer = (
        jnp.zeros((per_owner * owners * capacity, model_width), jnp.bfloat16)
        .at[slot_index]
        .set(moe_in)
    )
    send_buffer = send_buffer.reshape(per_owner, owners, capacity, model_width)
    w_in = expert_in[0, 0]
    w_out = expert_out[0, 0]
    by_group = shifted_exchange(send_buffer, "expert", 1)
    by_member = shifted_exchange(by_group, "z", 0)
    gathered = lax.all_gather(by_member, "y", axis=0, tiled=False)
    partial_out = expert_pass(gathered, w_in, w_out)
    returned = lax.all_to_all(partial_out, "y", split_axis=0, concat_axis=0, tiled=False)
    summed = jnp.sum(returned.astype(jnp.float32), axis=0).astype(jnp.bfloat16)
    results = shifted_exchange(summed, "z", 0, back=True)
    results = shifted_exchange(results, "expert", 1, back=True)
    frame_moe = results.reshape(-1, model_width)[slot_index]
    layer_out = mixed_res.astype(jnp.float32) + gate_value[:, None] * frame_moe.astype(jnp.float32)
    return layer_out.astype(jnp.bfloat16)[None]


def solution(mesh):
    tm_size = mesh.shape["tm"]
    y_size = QUARTERS
    split_mesh = Mesh(
        mesh.devices.reshape(tm_size // y_size, y_size, mesh.shape["expert"]), ("z", "y", "expert")
    )
    frames_spec = P("expert", ("z", "y"), None)
    weights_spec = P("expert", ("z", "y"), None, None)
    return jax.shard_map(
        shards,
        mesh=split_mesh,
        in_specs=(
            frames_spec,
            P("expert", None),
            frames_spec,
            P(),
            P(),
            P(),
            P(),
            P(),
            P(),
            weights_spec,
            weights_spec,
        ),
        out_specs=frames_spec,
        check_vma=False,
    )
```

```python
import jax
import jax.numpy as jnp
from jax import lax
from jax.sharding import Mesh, PartitionSpec as P

QUARTERS = 4
CHUNKS = 2


def padded_2(cells, sides, width):
    for axis, dim in sides:
        count = lax.axis_size(axis)
        ends = count - 1
        head = lax.slice_in_dim(cells, 0, width, axis=dim)
        tail = lax.slice_in_dim(cells, cells.shape[dim] - width, cells.shape[dim], axis=dim)
        cells = jnp.concatenate(
            [
                lax.ppermute(tail, axis, [(i, (i + 1) % count) for i in range(ends)]),
                cells,
                lax.ppermute(head, axis, [((i + 1) % count, i) for i in range(ends)]),
            ],
            axis=dim,
        )
    return cells


def shifted_exchange(blocks, axis, dim, back=False):
    count = lax.axis_size(axis)
    pieces = []
    for shift in range(count):
        piece = lax.index_in_dim(blocks, shift, axis=dim, keepdims=True)
        if shift:
            step = -shift if back else shift
            piece = lax.ppermute(piece, axis, [(i, (i + step) % count) for i in range(count)])
        pieces.append(piece)
    return jnp.concatenate(pieces, axis=dim)


def layer_norm(values):
    values = values.astype(jnp.float32)
    center = values - jnp.mean(values, axis=-1, keepdims=True)
    variance = jnp.mean(center * center, axis=-1, keepdims=True)
    return center * lax.rsqrt(variance + 1e-05)


def expert_pass(slot_block, w_in, w_out):
    slot_rows = slot_block.reshape(-1, slot_block.shape[-1])
    hidden = jax.nn.silu(jnp.dot(slot_rows, w_in, preferred_element_type=jnp.float32)).astype(
        jnp.bfloat16
    )
    partial_out = jnp.dot(hidden, w_out, preferred_element_type=jnp.float32).astype(jnp.bfloat16)
    return partial_out.reshape(slot_block.shape)


def shards(
    frames,
    utt_lengths,
    expert_ids,
    point_in,
    depth_taps,
    norm_scale,
    norm_shift,
    point_out,
    router,
    expert_in,
    expert_out,
):
    signal = frames[0]
    frame_count, model_width = signal.shape
    tap_count = depth_taps.shape[0]
    half_span = (tap_count - 1) // 2
    normed = layer_norm(signal).astype(jnp.bfloat16)
    projected = jnp.dot(normed, point_in, preferred_element_type=jnp.float32)
    gated_act = (projected[:, :model_width] * jax.nn.sigmoid(projected[:, model_width:])).astype(
        jnp.bfloat16
    )
    padded = padded_2(gated_act, ((("z", "y"), 0),), half_span)
    lengths = utt_lengths[0]
    utter_ends = jnp.cumsum(lengths, dtype=jnp.int32)
    utter_starts = utter_ends - lengths
    position = (lax.axis_index("z") * lax.axis_size("y") + lax.axis_index("y")) * frame_count + jnp.arange(frame_count, dtype=jnp.int32)
    inside = (utter_starts[None, :] <= position[:, None]) & (
        position[:, None] < utter_ends[None, :]
    )
    first_pos = jnp.sum(jnp.where(inside, utter_starts[None, :], 0), axis=1, dtype=jnp.int32)
    last_pos = jnp.sum(jnp.where(inside, utter_ends[None, :], 0), axis=1, dtype=jnp.int32)
    depth_sum = jnp.zeros((frame_count, model_width), jnp.float32)
    for tap_index in range(tap_count):
        nearby = position + (tap_index - half_span)
        inside_tap = ((nearby >= first_pos) & (nearby < last_pos)).astype(jnp.float32)
        window = padded[tap_index : tap_index + frame_count].astype(jnp.float32)
        depth_sum = depth_sum + depth_taps[tap_index][None, :] * window * inside_tap[:, None]
    activated = jax.nn.silu(depth_sum * norm_scale[None, :] + norm_shift[None, :]).astype(
        jnp.bfloat16
    )
    mixed_res = (
        signal.astype(jnp.float32)
        + jnp.dot(activated, point_out, preferred_element_type=jnp.float32)
    ).astype(jnp.bfloat16)
    moe_in = layer_norm(mixed_res).astype(jnp.bfloat16)
    route_ids = expert_ids[0, :, 0]
    expert_count = router.shape[1]
    capacity = 2 * frame_count // expert_count
    owners = lax.axis_size("expert")
    per_owner = expert_count // owners
    labels = jnp.arange(expert_count, dtype=jnp.int32)
    onehot = (route_ids[:, None] == labels[None, :]).astype(jnp.int32)
    earlier = jnp.cumsum(onehot, axis=0, dtype=jnp.int32) - onehot
    rank_in = jnp.sum(earlier * onehot, axis=1, dtype=jnp.int32)
    logits = jnp.dot(moe_in, router, preferred_element_type=jnp.float32)
    gate_value = jax.nn.sigmoid(jnp.sum(logits * onehot.astype(jnp.float32), axis=1))
    owner_group = (route_ids // per_owner - lax.axis_index("expert")) % owners
    member = (route_ids % per_owner - lax.axis_index("z")) % per_owner
    slot_index = (member * owners + owner_group) * capacity + rank_in
    send_buffer = (
        jnp.zeros((per_owner * owners * capacity, model_width), jnp.bfloat16)
        .at[slot_index]
        .set(moe_in)
    )
    send_buffer = send_buffer.reshape(per_owner, owners, capacity, model_width)
    w_in = expert_in[0, 0]
    w_out = expert_out[0, 0]
    chunk_results = []
    for chunk in jnp.split(send_buffer, CHUNKS, axis=2):
        by_group = shifted_exchange(chunk, "expert", 1)
        by_member = shifted_exchange(by_group, "z", 0)
        gathered = lax.all_gather(by_member, "y", axis=0, tiled=False)
        partial_out = expert_pass(gathered, w_in, w_out)
        returned = lax.all_to_all(partial_out, "y", split_axis=0, concat_axis=0, tiled=False)
        summed = jnp.sum(returned.astype(jnp.float32), axis=0).astype(jnp.bfloat16)
        back = shifted_exchange(summed, "z", 0, back=True)
        chunk_results.append(shifted_exchange(back, "expert", 1, back=True))
    results = jnp.concatenate(chunk_results, axis=2)
    frame_moe = results.reshape(-1, model_width)[slot_index]
    layer_out = mixed_res.astype(jnp.float32) + gate_value[:, None] * frame_moe.astype(jnp.float32)
    return layer_out.astype(jnp.bfloat16)[None]


def solution(mesh):
    tm_size = mesh.shape["tm"]
    y_size = QUARTERS
    split_mesh = Mesh(
        mesh.devices.reshape(tm_size // y_size, y_size, mesh.shape["expert"]), ("z", "y", "expert")
    )
    frames_spec = P("expert", ("z", "y"), None)
    weights_spec = P("expert", ("z", "y"), None, None)
    return jax.shard_map(
        shards,
        mesh=split_mesh,
        in_specs=(
            frames_spec,
            P("expert", None),
            frames_spec,
            P(),
            P(),
            P(),
            P(),
            P(),
            P(),
            weights_spec,
            weights_spec,
        ),
        out_specs=frames_spec,
        check_vma=False,
    )
```

```python
import jax
import jax.numpy as jnp
from jax import lax
from jax.sharding import Mesh, PartitionSpec as P

QUARTERS = 4


def padded_2(cells, sides, width):
    for axis, dim in sides:
        count = lax.axis_size(axis)
        ends = count - 1
        head = lax.slice_in_dim(cells, 0, width, axis=dim)
        tail = lax.slice_in_dim(cells, cells.shape[dim] - width, cells.shape[dim], axis=dim)
        cells = jnp.concatenate(
            [
                lax.ppermute(tail, axis, [(i, (i + 1) % count) for i in range(ends)]),
                cells,
                lax.ppermute(head, axis, [((i + 1) % count, i) for i in range(ends)]),
            ],
            axis=dim,
        )
    return cells


def layer_norm(values):
    values = values.astype(jnp.float32)
    center = values - jnp.mean(values, axis=-1, keepdims=True)
    variance = jnp.mean(center * center, axis=-1, keepdims=True)
    return center * lax.rsqrt(variance + 1e-05)


def expert_pass(slot_block, w_in, w_out):
    slot_rows = slot_block.reshape(-1, slot_block.shape[-1])
    hidden = jax.nn.silu(jnp.dot(slot_rows, w_in, preferred_element_type=jnp.float32)).astype(
        jnp.bfloat16
    )
    partial_out = jnp.dot(hidden, w_out, preferred_element_type=jnp.float32).astype(jnp.bfloat16)
    return partial_out.reshape(slot_block.shape)


def shards(
    frames,
    utt_lengths,
    expert_ids,
    point_in,
    depth_taps,
    norm_scale,
    norm_shift,
    point_out,
    router,
    expert_in,
    expert_out,
):
    signal = frames[0]
    frame_count, model_width = signal.shape
    tap_count = depth_taps.shape[0]
    half_span = (tap_count - 1) // 2
    normed = layer_norm(signal).astype(jnp.bfloat16)
    projected = jnp.dot(normed, point_in, preferred_element_type=jnp.float32)
    gated_act = (projected[:, :model_width] * jax.nn.sigmoid(projected[:, model_width:])).astype(
        jnp.bfloat16
    )
    padded = padded_2(gated_act, ((("z", "y"), 0),), half_span)
    lengths = utt_lengths[0]
    utter_ends = jnp.cumsum(lengths, dtype=jnp.int32)
    utter_starts = utter_ends - lengths
    position = (lax.axis_index("z") * lax.axis_size("y") + lax.axis_index("y")) * frame_count + jnp.arange(frame_count, dtype=jnp.int32)
    inside = (utter_starts[None, :] <= position[:, None]) & (
        position[:, None] < utter_ends[None, :]
    )
    first_pos = jnp.sum(jnp.where(inside, utter_starts[None, :], 0), axis=1, dtype=jnp.int32)
    last_pos = jnp.sum(jnp.where(inside, utter_ends[None, :], 0), axis=1, dtype=jnp.int32)
    depth_sum = jnp.zeros((frame_count, model_width), jnp.float32)
    for tap_index in range(tap_count):
        nearby = position + (tap_index - half_span)
        inside_tap = ((nearby >= first_pos) & (nearby < last_pos)).astype(jnp.float32)
        window = padded[tap_index : tap_index + frame_count].astype(jnp.float32)
        depth_sum = depth_sum + depth_taps[tap_index][None, :] * window * inside_tap[:, None]
    activated = jax.nn.silu(depth_sum * norm_scale[None, :] + norm_shift[None, :]).astype(
        jnp.bfloat16
    )
    mixed_res = (
        signal.astype(jnp.float32)
        + jnp.dot(activated, point_out, preferred_element_type=jnp.float32)
    ).astype(jnp.bfloat16)
    moe_in = layer_norm(mixed_res).astype(jnp.bfloat16)
    route_ids = expert_ids[0, :, 0]
    expert_count = router.shape[1]
    capacity = 2 * frame_count // expert_count
    owners = lax.axis_size("expert")
    per_owner = expert_count // owners
    labels = jnp.arange(expert_count, dtype=jnp.int32)
    onehot = (route_ids[:, None] == labels[None, :]).astype(jnp.int32)
    earlier = jnp.cumsum(onehot, axis=0, dtype=jnp.int32) - onehot
    rank_in = jnp.sum(earlier * onehot, axis=1, dtype=jnp.int32)
    logits = jnp.dot(moe_in, router, preferred_element_type=jnp.float32)
    gate_value = jax.nn.sigmoid(jnp.sum(logits * onehot.astype(jnp.float32), axis=1))
    owner_group = route_ids // per_owner
    member = route_ids % per_owner
    slot_index = (owner_group * per_owner + member) * capacity + rank_in
    send_buffer = (
        jnp.zeros((per_owner * owners * capacity, model_width), jnp.bfloat16)
        .at[slot_index]
        .set(moe_in)
    )
    send_buffer = send_buffer.reshape(owners * per_owner, capacity, model_width)
    w_in = expert_in[0, 0]
    w_out = expert_out[0, 0]
    by_member = lax.all_to_all(send_buffer, ("expert", "z"), split_axis=0, concat_axis=0, tiled=True)
    gathered = lax.all_gather(by_member, "y", axis=0, tiled=False)
    partial_out = expert_pass(gathered, w_in, w_out)
    returned = lax.all_to_all(partial_out, "y", split_axis=0, concat_axis=0, tiled=False)
    summed = jnp.sum(returned.astype(jnp.float32), axis=0).astype(jnp.bfloat16)
    results = lax.all_to_all(summed, ("expert", "z"), split_axis=0, concat_axis=0, tiled=True)
    frame_moe = results.reshape(-1, model_width)[slot_index]
    layer_out = mixed_res.astype(jnp.float32) + gate_value[:, None] * frame_moe.astype(jnp.float32)
    return layer_out.astype(jnp.bfloat16)[None]


def solution(mesh):
    tm_size = mesh.shape["tm"]
    y_size = QUARTERS
    split_mesh = Mesh(
        mesh.devices.reshape(tm_size // y_size, y_size, mesh.shape["expert"]), ("z", "y", "expert")
    )
    frames_spec = P("expert", ("z", "y"), None)
    weights_spec = P("expert", ("z", "y"), None, None)
    return jax.shard_map(
        shards,
        mesh=split_mesh,
        in_specs=(
            frames_spec,
            P("expert", None),
            frames_spec,
            P(),
            P(),
            P(),
            P(),
            P(),
            P(),
            weights_spec,
            weights_spec,
        ),
        out_specs=frames_spec,
        check_vma=False,
    )
```

```python
import jax
import jax.numpy as jnp
from jax import lax
from jax.sharding import Mesh, PartitionSpec as P

QUARTERS = 4


def padded_2(cells, sides, width):
    for axis, dim in sides:
        count = lax.axis_size(axis)
        ends = count - 1
        head = lax.slice_in_dim(cells, 0, width, axis=dim)
        tail = lax.slice_in_dim(cells, cells.shape[dim] - width, cells.shape[dim], axis=dim)
        cells = jnp.concatenate(
            [
                lax.ppermute(tail, axis, [(i, (i + 1) % count) for i in range(ends)]),
                cells,
                lax.ppermute(head, axis, [((i + 1) % count, i) for i in range(ends)]),
            ],
            axis=dim,
        )
    return cells


def layer_norm(values):
    values = values.astype(jnp.float32)
    center = values - jnp.mean(values, axis=-1, keepdims=True)
    variance = jnp.mean(center * center, axis=-1, keepdims=True)
    return center * lax.rsqrt(variance + 1e-05)


def expert_pass(slot_block, w_in, w_out):
    slot_rows = slot_block.reshape(-1, slot_block.shape[-1])
    hidden = jax.nn.silu(jnp.dot(slot_rows, w_in, preferred_element_type=jnp.float32)).astype(
        jnp.bfloat16
    )
    partial_out = jnp.dot(hidden, w_out, preferred_element_type=jnp.float32).astype(jnp.bfloat16)
    return partial_out.reshape(slot_block.shape)


def shards(
    frames,
    utt_lengths,
    expert_ids,
    point_in,
    depth_taps,
    norm_scale,
    norm_shift,
    point_out,
    router,
    expert_in,
    expert_out,
):
    signal = frames[0]
    frame_count, model_width = signal.shape
    tap_count = depth_taps.shape[0]
    half_span = (tap_count - 1) // 2
    normed = layer_norm(signal).astype(jnp.bfloat16)
    projected = jnp.dot(normed, point_in, preferred_element_type=jnp.float32)
    gated_act = (projected[:, :model_width] * jax.nn.sigmoid(projected[:, model_width:])).astype(
        jnp.bfloat16
    )
    padded = padded_2(gated_act, ((("z", "y"), 0),), half_span)
    lengths = utt_lengths[0]
    utter_ends = jnp.cumsum(lengths, dtype=jnp.int32)
    utter_starts = utter_ends - lengths
    position = (lax.axis_index("z") * lax.axis_size("y") + lax.axis_index("y")) * frame_count + jnp.arange(frame_count, dtype=jnp.int32)
    inside = (utter_starts[None, :] <= position[:, None]) & (
        position[:, None] < utter_ends[None, :]
    )
    first_pos = jnp.sum(jnp.where(inside, utter_starts[None, :], 0), axis=1, dtype=jnp.int32)
    last_pos = jnp.sum(jnp.where(inside, utter_ends[None, :], 0), axis=1, dtype=jnp.int32)
    depth_sum = jnp.zeros((frame_count, model_width), jnp.float32)
    for tap_index in range(tap_count):
        nearby = position + (tap_index - half_span)
        inside_tap = ((nearby >= first_pos) & (nearby < last_pos)).astype(jnp.float32)
        window = padded[tap_index : tap_index + frame_count].astype(jnp.float32)
        depth_sum = depth_sum + depth_taps[tap_index][None, :] * window * inside_tap[:, None]
    activated = jax.nn.silu(depth_sum * norm_scale[None, :] + norm_shift[None, :]).astype(
        jnp.bfloat16
    )
    mixed_res = (
        signal.astype(jnp.float32)
        + jnp.dot(activated, point_out, preferred_element_type=jnp.float32)
    ).astype(jnp.bfloat16)
    moe_in = layer_norm(mixed_res).astype(jnp.bfloat16)
    route_ids = expert_ids[0, :, 0]
    expert_count = router.shape[1]
    capacity = 2 * frame_count // expert_count
    owners = lax.axis_size("expert")
    per_owner = expert_count // owners
    labels = jnp.arange(expert_count, dtype=jnp.int32)
    onehot = (route_ids[:, None] == labels[None, :]).astype(jnp.int32)
    earlier = jnp.cumsum(onehot, axis=0, dtype=jnp.int32) - onehot
    rank_in = jnp.sum(earlier * onehot, axis=1, dtype=jnp.int32)
    logits = jnp.dot(moe_in, router, preferred_element_type=jnp.float32)
    gate_value = jax.nn.sigmoid(jnp.sum(logits * onehot.astype(jnp.float32), axis=1))
    owner_group = route_ids // per_owner
    member = route_ids % per_owner
    slot_index = (owner_group * per_owner + member) * capacity + rank_in
    send_buffer = (
        jnp.zeros((per_owner * owners * capacity, model_width), jnp.bfloat16)
        .at[slot_index]
        .set(moe_in)
    )
    send_buffer = send_buffer.reshape(owners * per_owner, capacity, model_width)
    w_in = expert_in[0, 0]
    w_out = expert_out[0, 0]
    by_member = lax.all_to_all(send_buffer, ("expert", "z"), split_axis=0, concat_axis=0, tiled=True)
    gathered = lax.all_gather(by_member, "y", axis=0, tiled=False)
    partial_out = expert_pass(gathered, w_in, w_out)
    summed = lax.psum_scatter(partial_out, "y", scatter_dimension=0, tiled=False)
    results = lax.all_to_all(summed, ("expert", "z"), split_axis=0, concat_axis=0, tiled=True)
    frame_moe = results.reshape(-1, model_width)[slot_index]
    layer_out = mixed_res.astype(jnp.float32) + gate_value[:, None] * frame_moe.astype(jnp.float32)
    return layer_out.astype(jnp.bfloat16)[None]


def solution(mesh):
    tm_size = mesh.shape["tm"]
    y_size = QUARTERS
    split_mesh = Mesh(
        mesh.devices.reshape(tm_size // y_size, y_size, mesh.shape["expert"]), ("z", "y", "expert")
    )
    frames_spec = P("expert", ("z", "y"), None)
    weights_spec = P("expert", ("z", "y"), None, None)
    return jax.shard_map(
        shards,
        mesh=split_mesh,
        in_specs=(
            frames_spec,
            P("expert", None),
            frames_spec,
            P(),
            P(),
            P(),
            P(),
            P(),
            P(),
            weights_spec,
            weights_spec,
        ),
        out_specs=frames_spec,
        check_vma=False,
    )
```

```python
import jax
import jax.numpy as jnp
from jax import lax
from jax.sharding import Mesh, PartitionSpec as P

QUARTERS = 4
CHUNKS = 2


def padded_2(cells, sides, width):
    for axis, dim in sides:
        count = lax.axis_size(axis)
        ends = count - 1
        head = lax.slice_in_dim(cells, 0, width, axis=dim)
        tail = lax.slice_in_dim(cells, cells.shape[dim] - width, cells.shape[dim], axis=dim)
        cells = jnp.concatenate(
            [
                lax.ppermute(tail, axis, [(i, (i + 1) % count) for i in range(ends)]),
                cells,
                lax.ppermute(head, axis, [((i + 1) % count, i) for i in range(ends)]),
            ],
            axis=dim,
        )
    return cells


def layer_norm(values):
    values = values.astype(jnp.float32)
    center = values - jnp.mean(values, axis=-1, keepdims=True)
    variance = jnp.mean(center * center, axis=-1, keepdims=True)
    return center * lax.rsqrt(variance + 1e-05)


def expert_pass(slot_block, w_in, w_out):
    slot_rows = slot_block.reshape(-1, slot_block.shape[-1])
    hidden = jax.nn.silu(jnp.dot(slot_rows, w_in, preferred_element_type=jnp.float32)).astype(
        jnp.bfloat16
    )
    partial_out = jnp.dot(hidden, w_out, preferred_element_type=jnp.float32).astype(jnp.bfloat16)
    return partial_out.reshape(slot_block.shape)


def shards(
    frames,
    utt_lengths,
    expert_ids,
    point_in,
    depth_taps,
    norm_scale,
    norm_shift,
    point_out,
    router,
    expert_in,
    expert_out,
):
    signal = frames[0]
    frame_count, model_width = signal.shape
    tap_count = depth_taps.shape[0]
    half_span = (tap_count - 1) // 2
    normed = layer_norm(signal).astype(jnp.bfloat16)
    projected = jnp.dot(normed, point_in, preferred_element_type=jnp.float32)
    gated_act = (projected[:, :model_width] * jax.nn.sigmoid(projected[:, model_width:])).astype(
        jnp.bfloat16
    )
    padded = padded_2(gated_act, ((("z", "y"), 0),), half_span)
    lengths = utt_lengths[0]
    utter_ends = jnp.cumsum(lengths, dtype=jnp.int32)
    utter_starts = utter_ends - lengths
    position = (lax.axis_index("z") * lax.axis_size("y") + lax.axis_index("y")) * frame_count + jnp.arange(frame_count, dtype=jnp.int32)
    inside = (utter_starts[None, :] <= position[:, None]) & (
        position[:, None] < utter_ends[None, :]
    )
    first_pos = jnp.sum(jnp.where(inside, utter_starts[None, :], 0), axis=1, dtype=jnp.int32)
    last_pos = jnp.sum(jnp.where(inside, utter_ends[None, :], 0), axis=1, dtype=jnp.int32)
    depth_sum = jnp.zeros((frame_count, model_width), jnp.float32)
    for tap_index in range(tap_count):
        nearby = position + (tap_index - half_span)
        inside_tap = ((nearby >= first_pos) & (nearby < last_pos)).astype(jnp.float32)
        window = padded[tap_index : tap_index + frame_count].astype(jnp.float32)
        depth_sum = depth_sum + depth_taps[tap_index][None, :] * window * inside_tap[:, None]
    activated = jax.nn.silu(depth_sum * norm_scale[None, :] + norm_shift[None, :]).astype(
        jnp.bfloat16
    )
    mixed_res = (
        signal.astype(jnp.float32)
        + jnp.dot(activated, point_out, preferred_element_type=jnp.float32)
    ).astype(jnp.bfloat16)
    moe_in = layer_norm(mixed_res).astype(jnp.bfloat16)
    route_ids = expert_ids[0, :, 0]
    expert_count = router.shape[1]
    capacity = 2 * frame_count // expert_count
    owners = lax.axis_size("expert")
    per_owner = expert_count // owners
    labels = jnp.arange(expert_count, dtype=jnp.int32)
    onehot = (route_ids[:, None] == labels[None, :]).astype(jnp.int32)
    earlier = jnp.cumsum(onehot, axis=0, dtype=jnp.int32) - onehot
    rank_in = jnp.sum(earlier * onehot, axis=1, dtype=jnp.int32)
    logits = jnp.dot(moe_in, router, preferred_element_type=jnp.float32)
    gate_value = jax.nn.sigmoid(jnp.sum(logits * onehot.astype(jnp.float32), axis=1))
    owner_group = route_ids // per_owner
    member = route_ids % per_owner
    slot_index = (owner_group * per_owner + member) * capacity + rank_in
    send_buffer = (
        jnp.zeros((per_owner * owners * capacity, model_width), jnp.bfloat16)
        .at[slot_index]
        .set(moe_in)
    )
    send_buffer = send_buffer.reshape(owners * per_owner, capacity, model_width)
    w_in = expert_in[0, 0]
    w_out = expert_out[0, 0]
    chunk_results = []
    for chunk in jnp.split(send_buffer, CHUNKS, axis=1):
        by_member = lax.all_to_all(chunk, ("expert", "z"), split_axis=0, concat_axis=0, tiled=True)
        gathered = lax.all_gather(by_member, "y", axis=0, tiled=False)
        partial_out = expert_pass(gathered, w_in, w_out)
        summed = lax.psum_scatter(partial_out, "y", scatter_dimension=0, tiled=False)
        chunk_results.append(
            lax.all_to_all(summed, ("expert", "z"), split_axis=0, concat_axis=0, tiled=True)
        )
    results = jnp.concatenate(chunk_results, axis=1)
    frame_moe = results.reshape(-1, model_width)[slot_index]
    layer_out = mixed_res.astype(jnp.float32) + gate_value[:, None] * frame_moe.astype(jnp.float32)
    return layer_out.astype(jnp.bfloat16)[None]


def solution(mesh):
    tm_size = mesh.shape["tm"]
    y_size = QUARTERS
    split_mesh = Mesh(
        mesh.devices.reshape(tm_size // y_size, y_size, mesh.shape["expert"]), ("z", "y", "expert")
    )
    frames_spec = P("expert", ("z", "y"), None)
    weights_spec = P("expert", ("z", "y"), None, None)
    return jax.shard_map(
        shards,
        mesh=split_mesh,
        in_specs=(
            frames_spec,
            P("expert", None),
            frames_spec,
            P(),
            P(),
            P(),
            P(),
            P(),
            P(),
            weights_spec,
            weights_spec,
        ),
        out_specs=frames_spec,
        check_vma=False,
    )
```

```python
import jax
import jax.numpy as jnp
from jax import lax
from jax.experimental import pallas as pl
from jax.experimental.pallas import tpu as pltpu
from jax.sharding import Mesh, PartitionSpec as P

QUARTERS = 4
ROW_BLOCK = 64
LANE_BLOCK = 128


def depthwise_kernel(pad_ref, taps_ref, first_ref, last_ref, scale_ref, shift_ref, out_ref, wide_ref):
    frame_count = out_ref.shape[0]
    tap_count = taps_ref.shape[0]
    half_span = (tap_count - 1) // 2
    wide_ref[...] = pad_ref[...].astype(jnp.float32)
    for row in range(0, frame_count, ROW_BLOCK):
        first_rel = first_ref[row : row + ROW_BLOCK, :]
        last_rel = last_ref[row : row + ROW_BLOCK, :]
        acc = jnp.zeros((ROW_BLOCK, out_ref.shape[1]), jnp.float32)
        for tap in range(tap_count):
            offset = tap - half_span
            valid = (first_rel <= offset) & (offset < last_rel)
            window = wide_ref[row + tap : row + tap + ROW_BLOCK, :]
            acc = acc + taps_ref[tap : tap + 1, :] * jnp.where(valid, window, 0.0)
        value = acc * scale_ref[...] + shift_ref[...]
        out_ref[row : row + ROW_BLOCK, :] = (value * jax.nn.sigmoid(value)).astype(out_ref.dtype)


def depthwise_silu(padded, taps, first_rel, last_rel, scale, shift):
    rows, width = padded.shape
    tap_count = taps.shape[0]
    frame_count = rows - (tap_count - 1)
    return pl.pallas_call(
        depthwise_kernel,
        grid=(width // LANE_BLOCK,),
        in_specs=[
            pl.BlockSpec((rows, LANE_BLOCK), lambda c: (0, c)),
            pl.BlockSpec((tap_count, LANE_BLOCK), lambda c: (0, c)),
            pl.BlockSpec((frame_count, 1), lambda c: (0, 0)),
            pl.BlockSpec((frame_count, 1), lambda c: (0, 0)),
            pl.BlockSpec((1, LANE_BLOCK), lambda c: (0, c)),
            pl.BlockSpec((1, LANE_BLOCK), lambda c: (0, c)),
        ],
        out_specs=pl.BlockSpec((frame_count, LANE_BLOCK), lambda c: (0, c)),
        out_shape=jax.ShapeDtypeStruct((frame_count, width), jnp.bfloat16),
        scratch_shapes=[pltpu.VMEM((rows, LANE_BLOCK), jnp.float32)],
    )(padded, taps, first_rel, last_rel, scale.reshape(1, -1), shift.reshape(1, -1))


def padded_2(cells, sides, width):
    for axis, dim in sides:
        count = lax.axis_size(axis)
        ends = count - 1
        head = lax.slice_in_dim(cells, 0, width, axis=dim)
        tail = lax.slice_in_dim(cells, cells.shape[dim] - width, cells.shape[dim], axis=dim)
        cells = jnp.concatenate(
            [
                lax.ppermute(tail, axis, [(i, (i + 1) % count) for i in range(ends)]),
                cells,
                lax.ppermute(head, axis, [((i + 1) % count, i) for i in range(ends)]),
            ],
            axis=dim,
        )
    return cells


def layer_norm(values):
    values = values.astype(jnp.float32)
    center = values - jnp.mean(values, axis=-1, keepdims=True)
    variance = jnp.mean(center * center, axis=-1, keepdims=True)
    return center * lax.rsqrt(variance + 1e-05)


def expert_pass(slot_block, w_in, w_out):
    slot_rows = slot_block.reshape(-1, slot_block.shape[-1])
    hidden = jax.nn.silu(jnp.dot(slot_rows, w_in, preferred_element_type=jnp.float32)).astype(
        jnp.bfloat16
    )
    partial_out = jnp.dot(hidden, w_out, preferred_element_type=jnp.float32).astype(jnp.bfloat16)
    return partial_out.reshape(slot_block.shape)


def shards(
    frames,
    utt_lengths,
    expert_ids,
    point_in,
    depth_taps,
    norm_scale,
    norm_shift,
    point_out,
    router,
    expert_in,
    expert_out,
):
    signal = frames[0]
    frame_count, model_width = signal.shape
    tap_count = depth_taps.shape[0]
    half_span = (tap_count - 1) // 2
    normed = layer_norm(signal).astype(jnp.bfloat16)
    projected = jnp.dot(normed, point_in, preferred_element_type=jnp.float32)
    gated_act = (projected[:, :model_width] * jax.nn.sigmoid(projected[:, model_width:])).astype(
        jnp.bfloat16
    )
    padded = padded_2(gated_act, ((("z", "y"), 0),), half_span)
    lengths = utt_lengths[0]
    utter_ends = jnp.cumsum(lengths, dtype=jnp.int32)
    utter_starts = utter_ends - lengths
    position = (lax.axis_index("z") * lax.axis_size("y") + lax.axis_index("y")) * frame_count + jnp.arange(frame_count, dtype=jnp.int32)
    inside = (utter_starts[None, :] <= position[:, None]) & (
        position[:, None] < utter_ends[None, :]
    )
    first_pos = jnp.sum(jnp.where(inside, utter_starts[None, :], 0), axis=1, dtype=jnp.int32)
    last_pos = jnp.sum(jnp.where(inside, utter_ends[None, :], 0), axis=1, dtype=jnp.int32)
    activated = depthwise_silu(
        padded,
        depth_taps,
        (first_pos - position)[:, None],
        (last_pos - position)[:, None],
        norm_scale,
        norm_shift,
    )
    mixed_res = (
        signal.astype(jnp.float32)
        + jnp.dot(activated, point_out, preferred_element_type=jnp.float32)
    ).astype(jnp.bfloat16)
    moe_in = layer_norm(mixed_res).astype(jnp.bfloat16)
    route_ids = expert_ids[0, :, 0]
    expert_count = router.shape[1]
    capacity = 2 * frame_count // expert_count
    owners = lax.axis_size("expert")
    per_owner = expert_count // owners
    labels = jnp.arange(expert_count, dtype=jnp.int32)
    onehot = (route_ids[:, None] == labels[None, :]).astype(jnp.int32)
    earlier = jnp.cumsum(onehot, axis=0, dtype=jnp.int32) - onehot
    rank_in = jnp.sum(earlier * onehot, axis=1, dtype=jnp.int32)
    logits = jnp.dot(moe_in, router, preferred_element_type=jnp.float32)
    gate_value = jax.nn.sigmoid(jnp.sum(logits * onehot.astype(jnp.float32), axis=1))
    owner_group = route_ids // per_owner
    member = route_ids % per_owner
    slot_index = (owner_group * per_owner + member) * capacity + rank_in
    send_buffer = (
        jnp.zeros((per_owner * owners * capacity, model_width), jnp.bfloat16)
        .at[slot_index]
        .set(moe_in)
    )
    send_buffer = send_buffer.reshape(owners * per_owner, capacity, model_width)
    w_in = expert_in[0, 0]
    w_out = expert_out[0, 0]
    by_member = lax.all_to_all(send_buffer, ("expert", "z"), split_axis=0, concat_axis=0, tiled=True)
    gathered = lax.all_gather(by_member, "y", axis=0, tiled=False)
    partial_out = expert_pass(gathered, w_in, w_out)
    summed = lax.psum_scatter(partial_out, "y", scatter_dimension=0, tiled=False)
    results = lax.all_to_all(summed, ("expert", "z"), split_axis=0, concat_axis=0, tiled=True)
    frame_moe = results.reshape(-1, model_width)[slot_index]
    layer_out = mixed_res.astype(jnp.float32) + gate_value[:, None] * frame_moe.astype(jnp.float32)
    return layer_out.astype(jnp.bfloat16)[None]


def solution(mesh):
    tm_size = mesh.shape["tm"]
    y_size = QUARTERS
    split_mesh = Mesh(
        mesh.devices.reshape(tm_size // y_size, y_size, mesh.shape["expert"]), ("z", "y", "expert")
    )
    frames_spec = P("expert", ("z", "y"), None)
    weights_spec = P("expert", ("z", "y"), None, None)
    return jax.shard_map(
        shards,
        mesh=split_mesh,
        in_specs=(
            frames_spec,
            P("expert", None),
            frames_spec,
            P(),
            P(),
            P(),
            P(),
            P(),
            P(),
            weights_spec,
            weights_spec,
        ),
        out_specs=frames_spec,
        check_vma=False,
    )
```

```python
import jax
import jax.numpy as jnp
from jax import lax
from jax.experimental import pallas as pl
from jax.experimental.pallas import tpu as pltpu
from jax.sharding import Mesh, PartitionSpec as P

QUARTERS = 4
CHUNKS = 2
ROW_BLOCK = 64
LANE_BLOCK = 128


def depthwise_kernel(pad_ref, taps_ref, first_ref, last_ref, scale_ref, shift_ref, out_ref, wide_ref):
    frame_count = out_ref.shape[0]
    tap_count = taps_ref.shape[0]
    half_span = (tap_count - 1) // 2
    wide_ref[...] = pad_ref[...].astype(jnp.float32)
    for row in range(0, frame_count, ROW_BLOCK):
        first_rel = first_ref[row : row + ROW_BLOCK, :]
        last_rel = last_ref[row : row + ROW_BLOCK, :]
        acc = jnp.zeros((ROW_BLOCK, out_ref.shape[1]), jnp.float32)
        for tap in range(tap_count):
            offset = tap - half_span
            valid = (first_rel <= offset) & (offset < last_rel)
            window = wide_ref[row + tap : row + tap + ROW_BLOCK, :]
            acc = acc + taps_ref[tap : tap + 1, :] * jnp.where(valid, window, 0.0)
        value = acc * scale_ref[...] + shift_ref[...]
        out_ref[row : row + ROW_BLOCK, :] = (value * jax.nn.sigmoid(value)).astype(out_ref.dtype)


def depthwise_silu(padded, taps, first_rel, last_rel, scale, shift):
    rows, width = padded.shape
    tap_count = taps.shape[0]
    frame_count = rows - (tap_count - 1)
    return pl.pallas_call(
        depthwise_kernel,
        grid=(width // LANE_BLOCK,),
        in_specs=[
            pl.BlockSpec((rows, LANE_BLOCK), lambda c: (0, c)),
            pl.BlockSpec((tap_count, LANE_BLOCK), lambda c: (0, c)),
            pl.BlockSpec((frame_count, 1), lambda c: (0, 0)),
            pl.BlockSpec((frame_count, 1), lambda c: (0, 0)),
            pl.BlockSpec((1, LANE_BLOCK), lambda c: (0, c)),
            pl.BlockSpec((1, LANE_BLOCK), lambda c: (0, c)),
        ],
        out_specs=pl.BlockSpec((frame_count, LANE_BLOCK), lambda c: (0, c)),
        out_shape=jax.ShapeDtypeStruct((frame_count, width), jnp.bfloat16),
        scratch_shapes=[pltpu.VMEM((rows, LANE_BLOCK), jnp.float32)],
    )(padded, taps, first_rel, last_rel, scale.reshape(1, -1), shift.reshape(1, -1))


def padded_2(cells, sides, width):
    for axis, dim in sides:
        count = lax.axis_size(axis)
        ends = count - 1
        head = lax.slice_in_dim(cells, 0, width, axis=dim)
        tail = lax.slice_in_dim(cells, cells.shape[dim] - width, cells.shape[dim], axis=dim)
        cells = jnp.concatenate(
            [
                lax.ppermute(tail, axis, [(i, (i + 1) % count) for i in range(ends)]),
                cells,
                lax.ppermute(head, axis, [((i + 1) % count, i) for i in range(ends)]),
            ],
            axis=dim,
        )
    return cells


def layer_norm(values):
    values = values.astype(jnp.float32)
    center = values - jnp.mean(values, axis=-1, keepdims=True)
    variance = jnp.mean(center * center, axis=-1, keepdims=True)
    return center * lax.rsqrt(variance + 1e-05)


def expert_pass(slot_block, w_in, w_out):
    slot_rows = slot_block.reshape(-1, slot_block.shape[-1])
    hidden = jax.nn.silu(jnp.dot(slot_rows, w_in, preferred_element_type=jnp.float32)).astype(
        jnp.bfloat16
    )
    partial_out = jnp.dot(hidden, w_out, preferred_element_type=jnp.float32).astype(jnp.bfloat16)
    return partial_out.reshape(slot_block.shape)


def shards(
    frames,
    utt_lengths,
    expert_ids,
    point_in,
    depth_taps,
    norm_scale,
    norm_shift,
    point_out,
    router,
    expert_in,
    expert_out,
):
    signal = frames[0]
    frame_count, model_width = signal.shape
    tap_count = depth_taps.shape[0]
    half_span = (tap_count - 1) // 2
    normed = layer_norm(signal).astype(jnp.bfloat16)
    projected = jnp.dot(normed, point_in, preferred_element_type=jnp.float32)
    gated_act = (projected[:, :model_width] * jax.nn.sigmoid(projected[:, model_width:])).astype(
        jnp.bfloat16
    )
    padded = padded_2(gated_act, ((("z", "y"), 0),), half_span)
    lengths = utt_lengths[0]
    utter_ends = jnp.cumsum(lengths, dtype=jnp.int32)
    utter_starts = utter_ends - lengths
    position = (lax.axis_index("z") * lax.axis_size("y") + lax.axis_index("y")) * frame_count + jnp.arange(frame_count, dtype=jnp.int32)
    inside = (utter_starts[None, :] <= position[:, None]) & (
        position[:, None] < utter_ends[None, :]
    )
    first_pos = jnp.sum(jnp.where(inside, utter_starts[None, :], 0), axis=1, dtype=jnp.int32)
    last_pos = jnp.sum(jnp.where(inside, utter_ends[None, :], 0), axis=1, dtype=jnp.int32)
    activated = depthwise_silu(
        padded,
        depth_taps,
        (first_pos - position)[:, None],
        (last_pos - position)[:, None],
        norm_scale,
        norm_shift,
    )
    mixed_res = (
        signal.astype(jnp.float32)
        + jnp.dot(activated, point_out, preferred_element_type=jnp.float32)
    ).astype(jnp.bfloat16)
    moe_in = layer_norm(mixed_res).astype(jnp.bfloat16)
    route_ids = expert_ids[0, :, 0]
    expert_count = router.shape[1]
    capacity = 2 * frame_count // expert_count
    owners = lax.axis_size("expert")
    per_owner = expert_count // owners
    labels = jnp.arange(expert_count, dtype=jnp.int32)
    onehot = (route_ids[:, None] == labels[None, :]).astype(jnp.int32)
    earlier = jnp.cumsum(onehot, axis=0, dtype=jnp.int32) - onehot
    rank_in = jnp.sum(earlier * onehot, axis=1, dtype=jnp.int32)
    logits = jnp.dot(moe_in, router, preferred_element_type=jnp.float32)
    gate_value = jax.nn.sigmoid(jnp.sum(logits * onehot.astype(jnp.float32), axis=1))
    owner_group = route_ids // per_owner
    member = route_ids % per_owner
    slot_index = rank_in * expert_count + owner_group * per_owner + member
    send_buffer = (
        jnp.zeros((per_owner * owners * capacity, model_width), jnp.bfloat16)
        .at[slot_index]
        .set(moe_in)
    )
    send_buffer = send_buffer.reshape(capacity, expert_count, model_width)
    w_in = expert_in[0, 0]
    w_out = expert_out[0, 0]
    chunk_results = []
    for chunk in jnp.split(send_buffer, CHUNKS, axis=0):
        by_member = lax.all_to_all(chunk, ("expert", "z"), split_axis=1, concat_axis=1, tiled=True)
        gathered = lax.all_gather(by_member, "y", axis=0, tiled=False)
        partial_out = expert_pass(gathered, w_in, w_out)
        summed = lax.psum_scatter(partial_out, "y", scatter_dimension=0, tiled=False)
        chunk_results.append(
            lax.all_to_all(summed, ("expert", "z"), split_axis=1, concat_axis=1, tiled=True)
        )
    results = jnp.concatenate(chunk_results, axis=0)
    frame_moe = results.reshape(-1, model_width)[slot_index]
    layer_out = mixed_res.astype(jnp.float32) + gate_value[:, None] * frame_moe.astype(jnp.float32)
    return layer_out.astype(jnp.bfloat16)[None]


def solution(mesh):
    tm_size = mesh.shape["tm"]
    y_size = QUARTERS
    split_mesh = Mesh(
        mesh.devices.reshape(tm_size // y_size, y_size, mesh.shape["expert"]), ("z", "y", "expert")
    )
    frames_spec = P("expert", ("z", "y"), None)
    weights_spec = P("expert", ("z", "y"), None, None)
    return jax.shard_map(
        shards,
        mesh=split_mesh,
        in_specs=(
            frames_spec,
            P("expert", None),
            frames_spec,
            P(),
            P(),
            P(),
            P(),
            P(),
            P(),
            weights_spec,
            weights_spec,
        ),
        out_specs=frames_spec,
        check_vma=False,
    )
```

```python
import jax
import jax.numpy as jnp
from jax import lax
from jax.experimental import pallas as pl
from jax.experimental.pallas import tpu as pltpu
from jax.sharding import Mesh, PartitionSpec as P

QUARTERS = 4
ROW_BLOCK = 64
LANE_BLOCK = 128


def depthwise_kernel(pad_ref, taps_ref, first_ref, last_ref, scale_ref, shift_ref, out_ref, wide_ref):
    frame_count = out_ref.shape[0]
    tap_count = taps_ref.shape[0]
    half_span = (tap_count - 1) // 2
    wide_ref[...] = pad_ref[...].astype(jnp.float32)
    for row in range(0, frame_count, ROW_BLOCK):
        first_rel = first_ref[row : row + ROW_BLOCK, :]
        last_rel = last_ref[row : row + ROW_BLOCK, :]
        acc = jnp.zeros((ROW_BLOCK, out_ref.shape[1]), jnp.float32)
        for tap in range(tap_count):
            offset = tap - half_span
            valid = (first_rel <= offset) & (offset < last_rel)
            window = wide_ref[row + tap : row + tap + ROW_BLOCK, :]
            acc = acc + taps_ref[tap : tap + 1, :] * jnp.where(valid, window, 0.0)
        value = acc * scale_ref[...] + shift_ref[...]
        out_ref[row : row + ROW_BLOCK, :] = (value * jax.nn.sigmoid(value)).astype(out_ref.dtype)


def depthwise_silu(padded, taps, first_rel, last_rel, scale, shift):
    rows, width = padded.shape
    tap_count = taps.shape[0]
    frame_count = rows - (tap_count - 1)
    return pl.pallas_call(
        depthwise_kernel,
        grid=(width // LANE_BLOCK,),
        in_specs=[
            pl.BlockSpec((rows, LANE_BLOCK), lambda c: (0, c)),
            pl.BlockSpec((tap_count, LANE_BLOCK), lambda c: (0, c)),
            pl.BlockSpec((frame_count, 1), lambda c: (0, 0)),
            pl.BlockSpec((frame_count, 1), lambda c: (0, 0)),
            pl.BlockSpec((1, LANE_BLOCK), lambda c: (0, c)),
            pl.BlockSpec((1, LANE_BLOCK), lambda c: (0, c)),
        ],
        out_specs=pl.BlockSpec((frame_count, LANE_BLOCK), lambda c: (0, c)),
        out_shape=jax.ShapeDtypeStruct((frame_count, width), jnp.bfloat16),
        scratch_shapes=[pltpu.VMEM((rows, LANE_BLOCK), jnp.float32)],
    )(padded, taps, first_rel, last_rel, scale.reshape(1, -1), shift.reshape(1, -1))


def halo_rows(cells, axis, width):
    count = lax.axis_size(axis)
    ends = count - 1
    head = cells[:width]
    tail = cells[cells.shape[0] - width :]
    return jnp.concatenate(
        [
            lax.ppermute(tail, axis, [(i, (i + 1) % count) for i in range(ends)]),
            lax.ppermute(head, axis, [((i + 1) % count, i) for i in range(ends)]),
        ],
        axis=0,
    )


def gated_unit(rows, point_in):
    model_width = rows.shape[1]
    normed = layer_norm(rows).astype(jnp.bfloat16)
    projected = jnp.dot(normed, point_in, preferred_element_type=jnp.float32)
    return (projected[:, :model_width] * jax.nn.sigmoid(projected[:, model_width:])).astype(
        jnp.bfloat16
    )


def layer_norm(values):
    values = values.astype(jnp.float32)
    center = values - jnp.mean(values, axis=-1, keepdims=True)
    variance = jnp.mean(center * center, axis=-1, keepdims=True)
    return center * lax.rsqrt(variance + 1e-05)


def expert_pass(slot_block, w_in, w_out):
    slot_rows = slot_block.reshape(-1, slot_block.shape[-1])
    hidden = jax.nn.silu(jnp.dot(slot_rows, w_in, preferred_element_type=jnp.float32)).astype(
        jnp.bfloat16
    )
    partial_out = jnp.dot(hidden, w_out, preferred_element_type=jnp.float32).astype(jnp.bfloat16)
    return partial_out.reshape(slot_block.shape)


def shards(
    frames,
    utt_lengths,
    expert_ids,
    point_in,
    depth_taps,
    norm_scale,
    norm_shift,
    point_out,
    router,
    expert_in,
    expert_out,
):
    signal = frames[0]
    frame_count, model_width = signal.shape
    tap_count = depth_taps.shape[0]
    half_span = (tap_count - 1) // 2
    halo = halo_rows(signal, ("z", "y"), half_span)
    gated_act = gated_unit(signal, point_in)
    gated_halo = gated_unit(halo, point_in)
    padded = jnp.concatenate(
        [gated_halo[:half_span], gated_act, gated_halo[half_span:]], axis=0
    )
    lengths = utt_lengths[0]
    utter_ends = jnp.cumsum(lengths, dtype=jnp.int32)
    utter_starts = utter_ends - lengths
    position = (lax.axis_index("z") * lax.axis_size("y") + lax.axis_index("y")) * frame_count + jnp.arange(frame_count, dtype=jnp.int32)
    inside = (utter_starts[None, :] <= position[:, None]) & (
        position[:, None] < utter_ends[None, :]
    )
    first_pos = jnp.sum(jnp.where(inside, utter_starts[None, :], 0), axis=1, dtype=jnp.int32)
    last_pos = jnp.sum(jnp.where(inside, utter_ends[None, :], 0), axis=1, dtype=jnp.int32)
    activated = depthwise_silu(
        padded,
        depth_taps,
        (first_pos - position)[:, None],
        (last_pos - position)[:, None],
        norm_scale,
        norm_shift,
    )
    mixed_res = (
        signal.astype(jnp.float32)
        + jnp.dot(activated, point_out, preferred_element_type=jnp.float32)
    ).astype(jnp.bfloat16)
    moe_in = layer_norm(mixed_res).astype(jnp.bfloat16)
    route_ids = expert_ids[0, :, 0]
    expert_count = router.shape[1]
    capacity = 2 * frame_count // expert_count
    owners = lax.axis_size("expert")
    per_owner = expert_count // owners
    labels = jnp.arange(expert_count, dtype=jnp.int32)
    onehot = (route_ids[:, None] == labels[None, :]).astype(jnp.int32)
    earlier = jnp.cumsum(onehot, axis=0, dtype=jnp.int32) - onehot
    rank_in = jnp.sum(earlier * onehot, axis=1, dtype=jnp.int32)
    logits = jnp.dot(moe_in, router, preferred_element_type=jnp.float32)
    gate_value = jax.nn.sigmoid(jnp.sum(logits * onehot.astype(jnp.float32), axis=1))
    owner_group = route_ids // per_owner
    member = route_ids % per_owner
    slot_index = (owner_group * per_owner + member) * capacity + rank_in
    send_buffer = (
        jnp.zeros((per_owner * owners * capacity, model_width), jnp.bfloat16)
        .at[slot_index]
        .set(moe_in)
    )
    send_buffer = send_buffer.reshape(owners * per_owner, capacity, model_width)
    w_in = expert_in[0, 0]
    w_out = expert_out[0, 0]
    by_member = lax.all_to_all(send_buffer, ("expert", "z"), split_axis=0, concat_axis=0, tiled=True)
    gathered = lax.all_gather(by_member, "y", axis=0, tiled=False)
    partial_out = expert_pass(gathered, w_in, w_out)
    summed = lax.psum_scatter(partial_out, "y", scatter_dimension=0, tiled=False)
    results = lax.all_to_all(summed, ("expert", "z"), split_axis=0, concat_axis=0, tiled=True)
    frame_moe = results.reshape(-1, model_width)[slot_index]
    layer_out = mixed_res.astype(jnp.float32) + gate_value[:, None] * frame_moe.astype(jnp.float32)
    return layer_out.astype(jnp.bfloat16)[None]


def solution(mesh):
    tm_size = mesh.shape["tm"]
    y_size = QUARTERS
    split_mesh = Mesh(
        mesh.devices.reshape(tm_size // y_size, y_size, mesh.shape["expert"]), ("z", "y", "expert")
    )
    frames_spec = P("expert", ("z", "y"), None)
    weights_spec = P("expert", ("z", "y"), None, None)
    return jax.shard_map(
        shards,
        mesh=split_mesh,
        in_specs=(
            frames_spec,
            P("expert", None),
            frames_spec,
            P(),
            P(),
            P(),
            P(),
            P(),
            P(),
            weights_spec,
            weights_spec,
        ),
        out_specs=frames_spec,
        check_vma=False,
    )
```

```python
import jax
import jax.numpy as jnp
from jax import lax
from jax.experimental import pallas as pl
from jax.experimental.pallas import tpu as pltpu
from jax.sharding import Mesh, PartitionSpec as P

QUARTERS = 4
ROW_BLOCK = 32
LANE_BLOCK = 512


def depthwise_kernel(pad_ref, taps_ref, first_ref, last_ref, scale_ref, shift_ref, out_ref, shifted_ref):
    frame_count = out_ref.shape[0]
    tap_count = taps_ref.shape[0]
    half_span = (tap_count - 1) // 2
    phases = 8
    span = shifted_ref.shape[1]
    for phase in range(phases):
        count = min(span, pad_ref.shape[0] - phase)
        shifted_ref[phase, :count, :] = pad_ref[phase : phase + count, :].astype(jnp.float32)
    for row in range(0, frame_count, ROW_BLOCK):
        first_rel = first_ref[row : row + ROW_BLOCK, :]
        last_rel = last_ref[row : row + ROW_BLOCK, :]
        acc = jnp.zeros((ROW_BLOCK, out_ref.shape[1]), jnp.float32)
        for tap in range(tap_count):
            offset = tap - half_span
            phase, base = tap % phases, tap - tap % phases
            window = shifted_ref[phase, row + base : row + base + ROW_BLOCK, :]
            valid = (first_rel <= offset) & (offset < last_rel)
            window = jnp.where(valid, window, 0.0)
            acc = acc + taps_ref[tap : tap + 1, :] * window
        value = acc * scale_ref[...] + shift_ref[...]
        out_ref[row : row + ROW_BLOCK, :] = (value * jax.nn.sigmoid(value)).astype(out_ref.dtype)


def depthwise_silu(padded, taps, first_rel, last_rel, scale, shift):
    rows, width = padded.shape
    tap_count = taps.shape[0]
    frame_count = rows - (tap_count - 1)
    span = frame_count + 24
    return pl.pallas_call(
        depthwise_kernel,
        grid=(width // LANE_BLOCK,),
        in_specs=[
            pl.BlockSpec((rows, LANE_BLOCK), lambda c: (0, c)),
            pl.BlockSpec((tap_count, LANE_BLOCK), lambda c: (0, c)),
            pl.BlockSpec((frame_count, 1), lambda c: (0, 0)),
            pl.BlockSpec((frame_count, 1), lambda c: (0, 0)),
            pl.BlockSpec((1, LANE_BLOCK), lambda c: (0, c)),
            pl.BlockSpec((1, LANE_BLOCK), lambda c: (0, c)),
        ],
        out_specs=pl.BlockSpec((frame_count, LANE_BLOCK), lambda c: (0, c)),
        out_shape=jax.ShapeDtypeStruct((frame_count, width), jnp.bfloat16),
        scratch_shapes=[pltpu.VMEM((8, span, LANE_BLOCK), jnp.float32)],
    )(padded, taps, first_rel, last_rel, scale.reshape(1, -1), shift.reshape(1, -1))


def padded_2(cells, sides, width):
    for axis, dim in sides:
        count = lax.axis_size(axis)
        ends = count - 1
        head = lax.slice_in_dim(cells, 0, width, axis=dim)
        tail = lax.slice_in_dim(cells, cells.shape[dim] - width, cells.shape[dim], axis=dim)
        cells = jnp.concatenate(
            [
                lax.ppermute(tail, axis, [(i, (i + 1) % count) for i in range(ends)]),
                cells,
                lax.ppermute(head, axis, [((i + 1) % count, i) for i in range(ends)]),
            ],
            axis=dim,
        )
    return cells


def layer_norm(values):
    values = values.astype(jnp.float32)
    center = values - jnp.mean(values, axis=-1, keepdims=True)
    variance = jnp.mean(center * center, axis=-1, keepdims=True)
    return center * lax.rsqrt(variance + 1e-05)


def expert_pass(slot_block, w_in, w_out):
    slot_rows = slot_block.reshape(-1, slot_block.shape[-1])
    hidden = jax.nn.silu(jnp.dot(slot_rows, w_in, preferred_element_type=jnp.float32)).astype(
        jnp.bfloat16
    )
    partial_out = jnp.dot(hidden, w_out, preferred_element_type=jnp.float32).astype(jnp.bfloat16)
    return partial_out.reshape(slot_block.shape)


def shards(
    frames,
    utt_lengths,
    expert_ids,
    point_in,
    depth_taps,
    norm_scale,
    norm_shift,
    point_out,
    router,
    expert_in,
    expert_out,
):
    signal = frames[0]
    frame_count, model_width = signal.shape
    tap_count = depth_taps.shape[0]
    half_span = (tap_count - 1) // 2
    normed = layer_norm(signal).astype(jnp.bfloat16)
    projected = jnp.dot(normed, point_in, preferred_element_type=jnp.float32)
    gated_act = (projected[:, :model_width] * jax.nn.sigmoid(projected[:, model_width:])).astype(
        jnp.bfloat16
    )
    padded = padded_2(gated_act, ((("z", "y"), 0),), half_span)
    lengths = utt_lengths[0]
    utter_ends = jnp.cumsum(lengths, dtype=jnp.int32)
    utter_starts = utter_ends - lengths
    position = (lax.axis_index("z") * lax.axis_size("y") + lax.axis_index("y")) * frame_count + jnp.arange(frame_count, dtype=jnp.int32)
    inside = (utter_starts[None, :] <= position[:, None]) & (
        position[:, None] < utter_ends[None, :]
    )
    first_pos = jnp.sum(jnp.where(inside, utter_starts[None, :], 0), axis=1, dtype=jnp.int32)
    last_pos = jnp.sum(jnp.where(inside, utter_ends[None, :], 0), axis=1, dtype=jnp.int32)
    activated = depthwise_silu(
        padded,
        depth_taps,
        (first_pos - position)[:, None],
        (last_pos - position)[:, None],
        norm_scale,
        norm_shift,
    )
    mixed_res = (
        signal.astype(jnp.float32)
        + jnp.dot(activated, point_out, preferred_element_type=jnp.float32)
    ).astype(jnp.bfloat16)
    moe_in = layer_norm(mixed_res).astype(jnp.bfloat16)
    route_ids = expert_ids[0, :, 0]
    expert_count = router.shape[1]
    capacity = 2 * frame_count // expert_count
    owners = lax.axis_size("expert")
    per_owner = expert_count // owners
    labels = jnp.arange(expert_count, dtype=jnp.int32)
    onehot = (route_ids[:, None] == labels[None, :]).astype(jnp.int32)
    earlier = jnp.cumsum(onehot, axis=0, dtype=jnp.int32) - onehot
    rank_in = jnp.sum(earlier * onehot, axis=1, dtype=jnp.int32)
    logits = jnp.dot(moe_in, router, preferred_element_type=jnp.float32)
    gate_value = jax.nn.sigmoid(jnp.sum(logits * onehot.astype(jnp.float32), axis=1))
    owner_group = route_ids // per_owner
    member = route_ids % per_owner
    slot_index = (owner_group * per_owner + member) * capacity + rank_in
    send_buffer = (
        jnp.zeros((per_owner * owners * capacity, model_width), jnp.bfloat16)
        .at[slot_index]
        .set(moe_in)
    )
    send_buffer = send_buffer.reshape(owners * per_owner, capacity, model_width)
    w_in = expert_in[0, 0]
    w_out = expert_out[0, 0]
    by_member = lax.all_to_all(send_buffer, ("expert", "z"), split_axis=0, concat_axis=0, tiled=True)
    gathered = lax.all_gather(by_member, "y", axis=0, tiled=False)
    partial_out = expert_pass(gathered, w_in, w_out)
    summed = lax.psum_scatter(partial_out, "y", scatter_dimension=0, tiled=False)
    results = lax.all_to_all(summed, ("expert", "z"), split_axis=0, concat_axis=0, tiled=True)
    frame_moe = results.reshape(-1, model_width)[slot_index]
    layer_out = mixed_res.astype(jnp.float32) + gate_value[:, None] * frame_moe.astype(jnp.float32)
    return layer_out.astype(jnp.bfloat16)[None]


def solution(mesh):
    tm_size = mesh.shape["tm"]
    y_size = QUARTERS
    split_mesh = Mesh(
        mesh.devices.reshape(tm_size // y_size, y_size, mesh.shape["expert"]), ("z", "y", "expert")
    )
    frames_spec = P("expert", ("z", "y"), None)
    weights_spec = P("expert", ("z", "y"), None, None)
    return jax.shard_map(
        shards,
        mesh=split_mesh,
        in_specs=(
            frames_spec,
            P("expert", None),
            frames_spec,
            P(),
            P(),
            P(),
            P(),
            P(),
            P(),
            weights_spec,
            weights_spec,
        ),
        out_specs=frames_spec,
        check_vma=False,
    )
```

```python
import jax
import jax.numpy as jnp
from jax import lax
from jax.experimental import pallas as pl
from jax.experimental.pallas import tpu as pltpu
from jax.sharding import Mesh, PartitionSpec as P

QUARTERS = 4
ROW_BLOCK = 32
LANE_BLOCK = 512


def depthwise_kernel(
    gated_ref,
    before_ref,
    after_ref,
    taps_ref,
    first_ref,
    last_ref,
    scale_ref,
    shift_ref,
    out_ref,
    wide_ref,
    shifted_ref,
):
    frame_count = out_ref.shape[0]
    tap_count = taps_ref.shape[0]
    half_span = (tap_count - 1) // 2
    phases = 8
    span = shifted_ref.shape[1]
    wide_ref[:half_span, :] = before_ref[...].astype(jnp.float32)
    wide_ref[half_span : half_span + frame_count, :] = gated_ref[...].astype(jnp.float32)
    wide_ref[half_span + frame_count :, :] = after_ref[...].astype(jnp.float32)
    for phase in range(phases):
        count = min(span, wide_ref.shape[0] - phase)
        shifted_ref[phase, :count, :] = wide_ref[phase : phase + count, :]
    for row in range(0, frame_count, ROW_BLOCK):
        first_rel = first_ref[row : row + ROW_BLOCK, :]
        last_rel = last_ref[row : row + ROW_BLOCK, :]
        acc = jnp.zeros((ROW_BLOCK, out_ref.shape[1]), jnp.float32)
        for tap in range(tap_count):
            offset = tap - half_span
            phase, base = tap % phases, tap - tap % phases
            window = shifted_ref[phase, row + base : row + base + ROW_BLOCK, :]
            valid = (first_rel <= offset) & (offset < last_rel)
            window = jnp.where(valid, window, 0.0)
            acc = acc + taps_ref[tap : tap + 1, :] * window
        value = acc * scale_ref[...] + shift_ref[...]
        out_ref[row : row + ROW_BLOCK, :] = (value * jax.nn.sigmoid(value)).astype(out_ref.dtype)


def depthwise_silu(gated, before, after, taps, first_rel, last_rel, scale, shift):
    frame_count, width = gated.shape
    tap_count = taps.shape[0]
    half_span = (tap_count - 1) // 2
    rows = frame_count + 2 * half_span
    span = frame_count + 24
    return pl.pallas_call(
        depthwise_kernel,
        grid=(width // LANE_BLOCK,),
        in_specs=[
            pl.BlockSpec((frame_count, LANE_BLOCK), lambda c: (0, c)),
            pl.BlockSpec((half_span, LANE_BLOCK), lambda c: (0, c)),
            pl.BlockSpec((half_span, LANE_BLOCK), lambda c: (0, c)),
            pl.BlockSpec((tap_count, LANE_BLOCK), lambda c: (0, c)),
            pl.BlockSpec((frame_count, 1), lambda c: (0, 0)),
            pl.BlockSpec((frame_count, 1), lambda c: (0, 0)),
            pl.BlockSpec((1, LANE_BLOCK), lambda c: (0, c)),
            pl.BlockSpec((1, LANE_BLOCK), lambda c: (0, c)),
        ],
        out_specs=pl.BlockSpec((frame_count, LANE_BLOCK), lambda c: (0, c)),
        out_shape=jax.ShapeDtypeStruct((frame_count, width), jnp.bfloat16),
        scratch_shapes=[
            pltpu.VMEM((rows, LANE_BLOCK), jnp.float32),
            pltpu.VMEM((8, span, LANE_BLOCK), jnp.float32),
        ],
    )(gated, before, after, taps, first_rel, last_rel, scale.reshape(1, -1), shift.reshape(1, -1))


def halo_pair(cells, axis, width):
    count = lax.axis_size(axis)
    ends = count - 1
    head = cells[:width]
    tail = cells[cells.shape[0] - width :]
    before = lax.ppermute(tail, axis, [(i, (i + 1) % count) for i in range(ends)])
    after = lax.ppermute(head, axis, [((i + 1) % count, i) for i in range(ends)])
    return before, after


def layer_norm(values):
    values = values.astype(jnp.float32)
    center = values - jnp.mean(values, axis=-1, keepdims=True)
    variance = jnp.mean(center * center, axis=-1, keepdims=True)
    return center * lax.rsqrt(variance + 1e-05)


def expert_pass(slot_block, w_in, w_out):
    slot_rows = slot_block.reshape(-1, slot_block.shape[-1])
    hidden = jax.nn.silu(jnp.dot(slot_rows, w_in, preferred_element_type=jnp.float32)).astype(
        jnp.bfloat16
    )
    partial_out = jnp.dot(hidden, w_out, preferred_element_type=jnp.float32).astype(jnp.bfloat16)
    return partial_out.reshape(slot_block.shape)


def shards(
    frames,
    utt_lengths,
    expert_ids,
    point_in,
    depth_taps,
    norm_scale,
    norm_shift,
    point_out,
    router,
    expert_in,
    expert_out,
):
    signal = frames[0]
    frame_count, model_width = signal.shape
    tap_count = depth_taps.shape[0]
    half_span = (tap_count - 1) // 2
    normed = layer_norm(signal).astype(jnp.bfloat16)
    projected = jnp.dot(normed, point_in, preferred_element_type=jnp.float32)
    gated_act = (projected[:, :model_width] * jax.nn.sigmoid(projected[:, model_width:])).astype(
        jnp.bfloat16
    )
    before, after = halo_pair(gated_act, ("z", "y"), half_span)
    lengths = utt_lengths[0]
    utter_ends = jnp.cumsum(lengths, dtype=jnp.int32)
    utter_starts = utter_ends - lengths
    position = (lax.axis_index("z") * lax.axis_size("y") + lax.axis_index("y")) * frame_count + jnp.arange(frame_count, dtype=jnp.int32)
    inside = (utter_starts[None, :] <= position[:, None]) & (
        position[:, None] < utter_ends[None, :]
    )
    first_pos = jnp.sum(jnp.where(inside, utter_starts[None, :], 0), axis=1, dtype=jnp.int32)
    last_pos = jnp.sum(jnp.where(inside, utter_ends[None, :], 0), axis=1, dtype=jnp.int32)
    activated = depthwise_silu(
        gated_act,
        before,
        after,
        depth_taps,
        (first_pos - position)[:, None],
        (last_pos - position)[:, None],
        norm_scale,
        norm_shift,
    )
    mixed_res = (
        signal.astype(jnp.float32)
        + jnp.dot(activated, point_out, preferred_element_type=jnp.float32)
    ).astype(jnp.bfloat16)
    moe_in = layer_norm(mixed_res).astype(jnp.bfloat16)
    route_ids = expert_ids[0, :, 0]
    expert_count = router.shape[1]
    capacity = 2 * frame_count // expert_count
    owners = lax.axis_size("expert")
    per_owner = expert_count // owners
    labels = jnp.arange(expert_count, dtype=jnp.int32)
    onehot = (route_ids[:, None] == labels[None, :]).astype(jnp.int32)
    earlier = jnp.cumsum(onehot, axis=0, dtype=jnp.int32) - onehot
    rank_in = jnp.sum(earlier * onehot, axis=1, dtype=jnp.int32)
    logits = jnp.dot(moe_in, router, preferred_element_type=jnp.float32)
    gate_value = jax.nn.sigmoid(jnp.sum(logits * onehot.astype(jnp.float32), axis=1))
    owner_group = route_ids // per_owner
    member = route_ids % per_owner
    slot_index = (owner_group * per_owner + member) * capacity + rank_in
    send_buffer = (
        jnp.zeros((per_owner * owners * capacity, model_width), jnp.bfloat16)
        .at[slot_index]
        .set(moe_in)
    )
    send_buffer = send_buffer.reshape(owners * per_owner, capacity, model_width)
    w_in = expert_in[0, 0]
    w_out = expert_out[0, 0]
    by_member = lax.all_to_all(send_buffer, ("expert", "z"), split_axis=0, concat_axis=0, tiled=True)
    gathered = lax.all_gather(by_member, "y", axis=0, tiled=False)
    partial_out = expert_pass(gathered, w_in, w_out)
    summed = lax.psum_scatter(partial_out, "y", scatter_dimension=0, tiled=False)
    results = lax.all_to_all(summed, ("expert", "z"), split_axis=0, concat_axis=0, tiled=True)
    frame_moe = results.reshape(-1, model_width)[slot_index]
    layer_out = mixed_res.astype(jnp.float32) + gate_value[:, None] * frame_moe.astype(jnp.float32)
    return layer_out.astype(jnp.bfloat16)[None]


def solution(mesh):
    tm_size = mesh.shape["tm"]
    y_size = QUARTERS
    split_mesh = Mesh(
        mesh.devices.reshape(tm_size // y_size, y_size, mesh.shape["expert"]), ("z", "y", "expert")
    )
    frames_spec = P("expert", ("z", "y"), None)
    weights_spec = P("expert", ("z", "y"), None, None)
    return jax.shard_map(
        shards,
        mesh=split_mesh,
        in_specs=(
            frames_spec,
            P("expert", None),
            frames_spec,
            P(),
            P(),
            P(),
            P(),
            P(),
            P(),
            weights_spec,
            weights_spec,
        ),
        out_specs=frames_spec,
        check_vma=False,
    )
```

```python
import jax
import jax.numpy as jnp
from jax import lax
from jax.experimental import pallas as pl
from jax.experimental.pallas import tpu as pltpu
from jax.sharding import Mesh, PartitionSpec as P

QUARTERS = 4
ROW_BLOCK = 32
LANE_BLOCK = 512


def depthwise_kernel(
    gated_ref,
    before_ref,
    after_ref,
    taps_ref,
    first_ref,
    last_ref,
    scale_ref,
    shift_ref,
    out_ref,
    wide_ref,
    shifted_ref,
):
    frame_count = out_ref.shape[0]
    tap_count = taps_ref.shape[0]
    half_span = (tap_count - 1) // 2
    phases = 8
    span = shifted_ref.shape[1]
    wide_ref[:half_span, :] = before_ref[...].astype(jnp.float32)
    wide_ref[half_span : half_span + frame_count, :] = gated_ref[...].astype(jnp.float32)
    wide_ref[half_span + frame_count :, :] = after_ref[...].astype(jnp.float32)
    for phase in range(phases):
        count = min(span, wide_ref.shape[0] - phase)
        shifted_ref[phase, :count, :] = wide_ref[phase : phase + count, :]
    for row in range(0, frame_count, ROW_BLOCK):
        first_rel = first_ref[row : row + ROW_BLOCK, :]
        last_rel = last_ref[row : row + ROW_BLOCK, :]
        acc = jnp.zeros((ROW_BLOCK, out_ref.shape[1]), jnp.float32)
        for tap in range(tap_count):
            offset = tap - half_span
            phase, base = tap % phases, tap - tap % phases
            window = shifted_ref[phase, row + base : row + base + ROW_BLOCK, :]
            valid = (first_rel <= offset) & (offset < last_rel)
            window = jnp.where(valid, window, 0.0)
            acc = acc + taps_ref[tap : tap + 1, :] * window
        value = acc * scale_ref[...] + shift_ref[...]
        out_ref[row : row + ROW_BLOCK, :] = (value * jax.nn.sigmoid(value)).astype(out_ref.dtype)


def depthwise_silu(gated, before, after, taps, first_rel, last_rel, scale, shift):
    frame_count, width = gated.shape
    tap_count = taps.shape[0]
    half_span = (tap_count - 1) // 2
    rows = frame_count + 2 * half_span
    span = frame_count + 24
    return pl.pallas_call(
        depthwise_kernel,
        grid=(width // LANE_BLOCK,),
        in_specs=[
            pl.BlockSpec((frame_count, LANE_BLOCK), lambda c: (0, c)),
            pl.BlockSpec((half_span, LANE_BLOCK), lambda c: (0, c)),
            pl.BlockSpec((half_span, LANE_BLOCK), lambda c: (0, c)),
            pl.BlockSpec((tap_count, LANE_BLOCK), lambda c: (0, c)),
            pl.BlockSpec((frame_count, 1), lambda c: (0, 0)),
            pl.BlockSpec((frame_count, 1), lambda c: (0, 0)),
            pl.BlockSpec((1, LANE_BLOCK), lambda c: (0, c)),
            pl.BlockSpec((1, LANE_BLOCK), lambda c: (0, c)),
        ],
        out_specs=pl.BlockSpec((frame_count, LANE_BLOCK), lambda c: (0, c)),
        out_shape=jax.ShapeDtypeStruct((frame_count, width), jnp.bfloat16),
        scratch_shapes=[
            pltpu.VMEM((rows, LANE_BLOCK), jnp.float32),
            pltpu.VMEM((8, span, LANE_BLOCK), jnp.float32),
        ],
    )(gated, before, after, taps, first_rel, last_rel, scale.reshape(1, -1), shift.reshape(1, -1))


def halo_pair(cells, axis, width):
    count = lax.axis_size(axis)
    ends = count - 1
    head = cells[:width]
    tail = cells[cells.shape[0] - width :]
    before = lax.ppermute(tail, axis, [(i, (i + 1) % count) for i in range(ends)])
    after = lax.ppermute(head, axis, [((i + 1) % count, i) for i in range(ends)])
    return before, after


def layer_norm(values):
    values = values.astype(jnp.float32)
    center = values - jnp.mean(values, axis=-1, keepdims=True)
    variance = jnp.mean(center * center, axis=-1, keepdims=True)
    return center * lax.rsqrt(variance + 1e-05)


def expert_pass(slot_block, w_in, w_out):
    slot_rows = slot_block.reshape(-1, slot_block.shape[-1])
    hidden = jax.nn.silu(jnp.dot(slot_rows, w_in, preferred_element_type=jnp.float32)).astype(
        jnp.bfloat16
    )
    partial_out = jnp.dot(hidden, w_out, preferred_element_type=jnp.float32).astype(jnp.bfloat16)
    return partial_out.reshape(slot_block.shape)


def shards(
    frames,
    utt_lengths,
    expert_ids,
    point_in,
    depth_taps,
    norm_scale,
    norm_shift,
    point_out,
    router,
    expert_in,
    expert_out,
):
    signal = frames[0]
    frame_count, model_width = signal.shape
    tap_count = depth_taps.shape[0]
    half_span = (tap_count - 1) // 2
    normed = layer_norm(signal).astype(jnp.bfloat16)
    projected = jnp.dot(normed, point_in, preferred_element_type=jnp.float32)
    gated_act = (projected[:, :model_width] * jax.nn.sigmoid(projected[:, model_width:])).astype(
        jnp.bfloat16
    )
    before, after = halo_pair(gated_act, ("z", "y"), half_span)
    lengths = utt_lengths[0]
    utter_ends = jnp.cumsum(lengths, dtype=jnp.int32)
    utter_starts = utter_ends - lengths
    position = (lax.axis_index("z") * lax.axis_size("y") + lax.axis_index("y")) * frame_count + jnp.arange(frame_count, dtype=jnp.int32)
    inside = (utter_starts[None, :] <= position[:, None]) & (
        position[:, None] < utter_ends[None, :]
    )
    first_pos = jnp.sum(jnp.where(inside, utter_starts[None, :], 0), axis=1, dtype=jnp.int32)
    last_pos = jnp.sum(jnp.where(inside, utter_ends[None, :], 0), axis=1, dtype=jnp.int32)
    activated = depthwise_silu(
        gated_act,
        before,
        after,
        depth_taps,
        (first_pos - position)[:, None],
        (last_pos - position)[:, None],
        norm_scale,
        norm_shift,
    )
    mixed_res = (
        signal.astype(jnp.float32)
        + jnp.dot(activated, point_out, preferred_element_type=jnp.float32)
    ).astype(jnp.bfloat16)
    moe_in = layer_norm(mixed_res).astype(jnp.bfloat16)
    route_ids = expert_ids[0, :, 0]
    expert_count = router.shape[1]
    capacity = 2 * frame_count // expert_count
    owners = lax.axis_size("expert")
    per_owner = expert_count // owners
    labels = jnp.arange(expert_count, dtype=jnp.int32)
    onehot = (route_ids[:, None] == labels[None, :]).astype(jnp.int32)
    earlier = jnp.cumsum(onehot, axis=0, dtype=jnp.int32) - onehot
    rank_in = jnp.sum(earlier * onehot, axis=1, dtype=jnp.int32)
    logits = jnp.dot(moe_in, router, preferred_element_type=jnp.float32)
    gate_value = jax.nn.sigmoid(jnp.sum(logits * onehot.astype(jnp.float32), axis=1))
    owner_group = route_ids // per_owner
    member = route_ids % per_owner
    slot_index = (owner_group * per_owner + member) * capacity + rank_in
    slot_count = per_owner * owners * capacity
    placing = (slot_index[:, None] == jnp.arange(slot_count, dtype=jnp.int32)[None, :]).astype(
        jnp.bfloat16
    )
    send_buffer = lax.dot_general(
        placing, moe_in, (((0,), (0,)), ((), ())), preferred_element_type=jnp.float32
    ).astype(jnp.bfloat16)
    send_buffer = send_buffer.reshape(owners * per_owner, capacity, model_width)
    w_in = expert_in[0, 0]
    w_out = expert_out[0, 0]
    by_member = lax.all_to_all(send_buffer, ("expert", "z"), split_axis=0, concat_axis=0, tiled=True)
    gathered = lax.all_gather(by_member, "y", axis=0, tiled=False)
    partial_out = expert_pass(gathered, w_in, w_out)
    summed = lax.psum_scatter(partial_out, "y", scatter_dimension=0, tiled=False)
    results = lax.all_to_all(summed, ("expert", "z"), split_axis=0, concat_axis=0, tiled=True)
    frame_moe = jnp.dot(
        placing, results.reshape(-1, model_width), preferred_element_type=jnp.float32
    )
    layer_out = mixed_res.astype(jnp.float32) + gate_value[:, None] * frame_moe.astype(jnp.float32)
    return layer_out.astype(jnp.bfloat16)[None]


def solution(mesh):
    tm_size = mesh.shape["tm"]
    y_size = QUARTERS
    split_mesh = Mesh(
        mesh.devices.reshape(tm_size // y_size, y_size, mesh.shape["expert"]), ("z", "y", "expert")
    )
    frames_spec = P("expert", ("z", "y"), None)
    weights_spec = P("expert", ("z", "y"), None, None)
    return jax.shard_map(
        shards,
        mesh=split_mesh,
        in_specs=(
            frames_spec,
            P("expert", None),
            frames_spec,
            P(),
            P(),
            P(),
            P(),
            P(),
            P(),
            weights_spec,
            weights_spec,
        ),
        out_specs=frames_spec,
        check_vma=False,
    )
```

```python
import jax
import jax.numpy as jnp
from jax import lax
from jax.experimental import pallas as pl
from jax.experimental.pallas import tpu as pltpu
from jax.sharding import Mesh, PartitionSpec as P

QUARTERS = 4
ROW_BLOCK = 32
LANE_BLOCK = 512
ROW_TILE = 512


def depthwise_kernel(
    gated_ref,
    before_ref,
    after_ref,
    taps_ref,
    first_ref,
    last_ref,
    scale_ref,
    shift_ref,
    out_ref,
    wide_ref,
    shifted_ref,
):
    frame_count = out_ref.shape[0]
    tap_count = taps_ref.shape[0]
    half_span = (tap_count - 1) // 2
    phases = 8
    span = shifted_ref.shape[1]
    wide_ref[:half_span, :] = before_ref[...].astype(jnp.float32)
    wide_ref[half_span : half_span + frame_count, :] = gated_ref[...].astype(jnp.float32)
    wide_ref[half_span + frame_count :, :] = after_ref[...].astype(jnp.float32)
    for phase in range(phases):
        count = min(span, wide_ref.shape[0] - phase)
        shifted_ref[phase, :count, :] = wide_ref[phase : phase + count, :]
    for row in range(0, frame_count, ROW_BLOCK):
        first_rel = first_ref[row : row + ROW_BLOCK, :]
        last_rel = last_ref[row : row + ROW_BLOCK, :]
        acc = jnp.zeros((ROW_BLOCK, out_ref.shape[1]), jnp.float32)
        for tap in range(tap_count):
            offset = tap - half_span
            phase, base = tap % phases, tap - tap % phases
            window = shifted_ref[phase, row + base : row + base + ROW_BLOCK, :]
            valid = (first_rel <= offset) & (offset < last_rel)
            window = jnp.where(valid, window, 0.0)
            acc = acc + taps_ref[tap : tap + 1, :] * window
        value = acc * scale_ref[...] + shift_ref[...]
        out_ref[row : row + ROW_BLOCK, :] = (value * jax.nn.sigmoid(value)).astype(out_ref.dtype)


def depthwise_silu(gated, before, after, taps, first_rel, last_rel, scale, shift):
    frame_count, width = gated.shape
    tap_count = taps.shape[0]
    half_span = (tap_count - 1) // 2
    rows = frame_count + 2 * half_span
    span = frame_count + 24
    return pl.pallas_call(
        depthwise_kernel,
        grid=(width // LANE_BLOCK,),
        in_specs=[
            pl.BlockSpec((frame_count, LANE_BLOCK), lambda c: (0, c)),
            pl.BlockSpec((half_span, LANE_BLOCK), lambda c: (0, c)),
            pl.BlockSpec((half_span, LANE_BLOCK), lambda c: (0, c)),
            pl.BlockSpec((tap_count, LANE_BLOCK), lambda c: (0, c)),
            pl.BlockSpec((frame_count, 1), lambda c: (0, 0)),
            pl.BlockSpec((frame_count, 1), lambda c: (0, 0)),
            pl.BlockSpec((1, LANE_BLOCK), lambda c: (0, c)),
            pl.BlockSpec((1, LANE_BLOCK), lambda c: (0, c)),
        ],
        out_specs=pl.BlockSpec((frame_count, LANE_BLOCK), lambda c: (0, c)),
        out_shape=jax.ShapeDtypeStruct((frame_count, width), jnp.bfloat16),
        scratch_shapes=[
            pltpu.VMEM((rows, LANE_BLOCK), jnp.float32),
            pltpu.VMEM((8, span, LANE_BLOCK), jnp.float32),
        ],
    )(gated, before, after, taps, first_rel, last_rel, scale.reshape(1, -1), shift.reshape(1, -1))


def halo_pair(cells, axis, width):
    count = lax.axis_size(axis)
    ends = count - 1
    head = cells[:width]
    tail = cells[cells.shape[0] - width :]
    before = lax.ppermute(tail, axis, [(i, (i + 1) % count) for i in range(ends)])
    after = lax.ppermute(head, axis, [((i + 1) % count, i) for i in range(ends)])
    return before, after


def layer_norm(values):
    values = values.astype(jnp.float32)
    center = values - jnp.mean(values, axis=-1, keepdims=True)
    variance = jnp.mean(center * center, axis=-1, keepdims=True)
    return center * lax.rsqrt(variance + 1e-05)


def expert_kernel(rows_ref, w_in_ref, w_out_ref, out_ref):
    hidden = jnp.dot(rows_ref[...], w_in_ref[...], preferred_element_type=jnp.float32)
    hidden = (hidden * jax.nn.sigmoid(hidden)).astype(jnp.bfloat16)
    out_ref[...] = jnp.dot(hidden, w_out_ref[...], preferred_element_type=jnp.float32).astype(
        out_ref.dtype
    )


def expert_pass(slot_block, w_in, w_out):
    slot_rows = slot_block.reshape(-1, slot_block.shape[-1])
    row_count, model_width = slot_rows.shape
    hidden_width = w_in.shape[1]
    tile = min(ROW_TILE, row_count)
    partial_out = pl.pallas_call(
        expert_kernel,
        grid=(row_count // tile,),
        in_specs=[
            pl.BlockSpec((tile, model_width), lambda r: (r, 0)),
            pl.BlockSpec((model_width, hidden_width), lambda r: (0, 0)),
            pl.BlockSpec((hidden_width, model_width), lambda r: (0, 0)),
        ],
        out_specs=pl.BlockSpec((tile, model_width), lambda r: (r, 0)),
        out_shape=jax.ShapeDtypeStruct((row_count, model_width), jnp.bfloat16),
    )(slot_rows, w_in, w_out)
    return partial_out.reshape(slot_block.shape)


def shards(
    frames,
    utt_lengths,
    expert_ids,
    point_in,
    depth_taps,
    norm_scale,
    norm_shift,
    point_out,
    router,
    expert_in,
    expert_out,
):
    signal = frames[0]
    frame_count, model_width = signal.shape
    tap_count = depth_taps.shape[0]
    half_span = (tap_count - 1) // 2
    normed = layer_norm(signal).astype(jnp.bfloat16)
    projected = jnp.dot(normed, point_in, preferred_element_type=jnp.float32)
    gated_act = (projected[:, :model_width] * jax.nn.sigmoid(projected[:, model_width:])).astype(
        jnp.bfloat16
    )
    before, after = halo_pair(gated_act, ("z", "y"), half_span)
    lengths = utt_lengths[0]
    utter_ends = jnp.cumsum(lengths, dtype=jnp.int32)
    utter_starts = utter_ends - lengths
    position = (lax.axis_index("z") * lax.axis_size("y") + lax.axis_index("y")) * frame_count + jnp.arange(frame_count, dtype=jnp.int32)
    inside = (utter_starts[None, :] <= position[:, None]) & (
        position[:, None] < utter_ends[None, :]
    )
    first_pos = jnp.sum(jnp.where(inside, utter_starts[None, :], 0), axis=1, dtype=jnp.int32)
    last_pos = jnp.sum(jnp.where(inside, utter_ends[None, :], 0), axis=1, dtype=jnp.int32)
    activated = depthwise_silu(
        gated_act,
        before,
        after,
        depth_taps,
        (first_pos - position)[:, None],
        (last_pos - position)[:, None],
        norm_scale,
        norm_shift,
    )
    mixed_res = (
        signal.astype(jnp.float32)
        + jnp.dot(activated, point_out, preferred_element_type=jnp.float32)
    ).astype(jnp.bfloat16)
    moe_in = layer_norm(mixed_res).astype(jnp.bfloat16)
    route_ids = expert_ids[0, :, 0]
    expert_count = router.shape[1]
    capacity = 2 * frame_count // expert_count
    owners = lax.axis_size("expert")
    per_owner = expert_count // owners
    labels = jnp.arange(expert_count, dtype=jnp.int32)
    onehot = (route_ids[:, None] == labels[None, :]).astype(jnp.int32)
    earlier = jnp.cumsum(onehot, axis=0, dtype=jnp.int32) - onehot
    rank_in = jnp.sum(earlier * onehot, axis=1, dtype=jnp.int32)
    logits = jnp.dot(moe_in, router, preferred_element_type=jnp.float32)
    gate_value = jax.nn.sigmoid(jnp.sum(logits * onehot.astype(jnp.float32), axis=1))
    owner_group = route_ids // per_owner
    member = route_ids % per_owner
    slot_index = (owner_group * per_owner + member) * capacity + rank_in
    slot_count = per_owner * owners * capacity
    placing = (slot_index[:, None] == jnp.arange(slot_count, dtype=jnp.int32)[None, :]).astype(
        jnp.bfloat16
    )
    send_buffer = lax.dot_general(
        placing, moe_in, (((0,), (0,)), ((), ())), preferred_element_type=jnp.float32
    ).astype(jnp.bfloat16)
    send_buffer = send_buffer.reshape(owners * per_owner, capacity, model_width)
    w_in = expert_in[0, 0]
    w_out = expert_out[0, 0]
    by_member = lax.all_to_all(send_buffer, ("expert", "z"), split_axis=0, concat_axis=0, tiled=True)
    gathered = lax.all_gather(by_member, "y", axis=0, tiled=False)
    partial_out = expert_pass(gathered, w_in, w_out)
    summed = lax.psum_scatter(partial_out, "y", scatter_dimension=0, tiled=False)
    results = lax.all_to_all(summed, ("expert", "z"), split_axis=0, concat_axis=0, tiled=True)
    frame_moe = jnp.dot(
        placing, results.reshape(-1, model_width), preferred_element_type=jnp.float32
    )
    layer_out = mixed_res.astype(jnp.float32) + gate_value[:, None] * frame_moe.astype(jnp.float32)
    return layer_out.astype(jnp.bfloat16)[None]


def solution(mesh):
    tm_size = mesh.shape["tm"]
    y_size = QUARTERS
    split_mesh = Mesh(
        mesh.devices.reshape(tm_size // y_size, y_size, mesh.shape["expert"]), ("z", "y", "expert")
    )
    frames_spec = P("expert", ("z", "y"), None)
    weights_spec = P("expert", ("z", "y"), None, None)
    return jax.shard_map(
        shards,
        mesh=split_mesh,
        in_specs=(
            frames_spec,
            P("expert", None),
            frames_spec,
            P(),
            P(),
            P(),
            P(),
            P(),
            P(),
            weights_spec,
            weights_spec,
        ),
        out_specs=frames_spec,
        check_vma=False,
    )
```

```python
import jax
import jax.numpy as jnp
from jax import lax
from jax.experimental import pallas as pl
from jax.experimental.pallas import tpu as pltpu
from jax.sharding import Mesh, PartitionSpec as P

QUARTERS = 4
ROW_BLOCK = 32
LANE_BLOCK = 512
ROW_TILE = 512


def depthwise_kernel(
    gated_ref,
    before_ref,
    after_ref,
    taps_ref,
    first_ref,
    last_ref,
    scale_ref,
    shift_ref,
    out_ref,
    wide_ref,
    shifted_ref,
):
    frame_count = out_ref.shape[0]
    tap_count = taps_ref.shape[0]
    half_span = (tap_count - 1) // 2
    phases = 8
    span = shifted_ref.shape[1]
    wide_ref[:half_span, :] = before_ref[...].astype(jnp.float32)
    wide_ref[half_span : half_span + frame_count, :] = gated_ref[...].astype(jnp.float32)
    wide_ref[half_span + frame_count :, :] = after_ref[...].astype(jnp.float32)
    for phase in range(phases):
        count = min(span, wide_ref.shape[0] - phase)
        shifted_ref[phase, :count, :] = wide_ref[phase : phase + count, :]
    for row in range(0, frame_count, ROW_BLOCK):
        first_rel = first_ref[row : row + ROW_BLOCK, :]
        last_rel = last_ref[row : row + ROW_BLOCK, :]
        acc = jnp.zeros((ROW_BLOCK, out_ref.shape[1]), jnp.float32)
        for tap in range(tap_count):
            offset = tap - half_span
            phase, base = tap % phases, tap - tap % phases
            window = shifted_ref[phase, row + base : row + base + ROW_BLOCK, :]
            valid = (first_rel <= offset) & (offset < last_rel)
            window = jnp.where(valid, window, 0.0)
            acc = acc + taps_ref[tap : tap + 1, :] * window
        value = acc * scale_ref[...] + shift_ref[...]
        out_ref[row : row + ROW_BLOCK, :] = (value * jax.nn.sigmoid(value)).astype(out_ref.dtype)


def depthwise_silu(gated, before, after, taps, first_rel, last_rel, scale, shift):
    frame_count, width = gated.shape
    tap_count = taps.shape[0]
    half_span = (tap_count - 1) // 2
    rows = frame_count + 2 * half_span
    span = frame_count + 24
    return pl.pallas_call(
        depthwise_kernel,
        grid=(width // LANE_BLOCK,),
        in_specs=[
            pl.BlockSpec((frame_count, LANE_BLOCK), lambda c: (0, c)),
            pl.BlockSpec((half_span, LANE_BLOCK), lambda c: (0, c)),
            pl.BlockSpec((half_span, LANE_BLOCK), lambda c: (0, c)),
            pl.BlockSpec((tap_count, LANE_BLOCK), lambda c: (0, c)),
            pl.BlockSpec((frame_count, 1), lambda c: (0, 0)),
            pl.BlockSpec((frame_count, 1), lambda c: (0, 0)),
            pl.BlockSpec((1, LANE_BLOCK), lambda c: (0, c)),
            pl.BlockSpec((1, LANE_BLOCK), lambda c: (0, c)),
        ],
        out_specs=pl.BlockSpec((frame_count, LANE_BLOCK), lambda c: (0, c)),
        out_shape=jax.ShapeDtypeStruct((frame_count, width), jnp.bfloat16),
        scratch_shapes=[
            pltpu.VMEM((rows, LANE_BLOCK), jnp.float32),
            pltpu.VMEM((8, span, LANE_BLOCK), jnp.float32),
        ],
    )(gated, before, after, taps, first_rel, last_rel, scale.reshape(1, -1), shift.reshape(1, -1))


def halo_pair(cells, axis, width):
    count = lax.axis_size(axis)
    ends = count - 1
    head = cells[:width]
    tail = cells[cells.shape[0] - width :]
    before = lax.ppermute(tail, axis, [(i, (i + 1) % count) for i in range(ends)])
    after = lax.ppermute(head, axis, [((i + 1) % count, i) for i in range(ends)])
    return before, after


def layer_norm(values):
    values = values.astype(jnp.float32)
    center = values - jnp.mean(values, axis=-1, keepdims=True)
    variance = jnp.mean(center * center, axis=-1, keepdims=True)
    return center * lax.rsqrt(variance + 1e-05)


def expert_kernel(rows_ref, w_in_ref, w_out_ref, out_ref):
    hidden = jnp.dot(rows_ref[...], w_in_ref[...], preferred_element_type=jnp.float32)
    hidden = (hidden * jax.nn.sigmoid(hidden)).astype(jnp.bfloat16)
    out_ref[...] = jnp.dot(hidden, w_out_ref[...], preferred_element_type=jnp.float32).astype(
        out_ref.dtype
    )


def expert_pass(slot_block, w_in, w_out):
    slot_rows = slot_block.reshape(-1, slot_block.shape[-1])
    row_count, model_width = slot_rows.shape
    hidden_width = w_in.shape[1]
    tile = min(ROW_TILE, row_count)
    partial_out = pl.pallas_call(
        expert_kernel,
        grid=(row_count // tile,),
        in_specs=[
            pl.BlockSpec((tile, model_width), lambda r: (r, 0)),
            pl.BlockSpec((model_width, hidden_width), lambda r: (0, 0)),
            pl.BlockSpec((hidden_width, model_width), lambda r: (0, 0)),
        ],
        out_specs=pl.BlockSpec((tile, model_width), lambda r: (r, 0)),
        out_shape=jax.ShapeDtypeStruct((row_count, model_width), jnp.bfloat16),
    )(slot_rows, w_in, w_out)
    return partial_out.reshape(slot_block.shape)


def shards(
    frames,
    utt_lengths,
    expert_ids,
    point_in,
    depth_taps,
    norm_scale,
    norm_shift,
    point_out,
    router,
    expert_in,
    expert_out,
):
    signal = frames[0]
    frame_count, model_width = signal.shape
    tap_count = depth_taps.shape[0]
    half_span = (tap_count - 1) // 2
    normed = layer_norm(signal).astype(jnp.bfloat16)
    projected = jnp.dot(normed, point_in, preferred_element_type=jnp.float32)
    gated_act = (projected[:, :model_width] * jax.nn.sigmoid(projected[:, model_width:])).astype(
        jnp.bfloat16
    )
    before, after = halo_pair(gated_act, ("z", "y"), half_span)
    lengths = utt_lengths[0]
    utter_ends = jnp.cumsum(lengths, dtype=jnp.int32)
    utter_starts = utter_ends - lengths
    position = (lax.axis_index("z") * lax.axis_size("y") + lax.axis_index("y")) * frame_count + jnp.arange(frame_count, dtype=jnp.int32)
    inside = (utter_starts[None, :] <= position[:, None]) & (
        position[:, None] < utter_ends[None, :]
    )
    first_pos = jnp.sum(jnp.where(inside, utter_starts[None, :], 0), axis=1, dtype=jnp.int32)
    last_pos = jnp.sum(jnp.where(inside, utter_ends[None, :], 0), axis=1, dtype=jnp.int32)
    activated = depthwise_silu(
        gated_act,
        before,
        after,
        depth_taps,
        (first_pos - position)[:, None],
        (last_pos - position)[:, None],
        norm_scale,
        norm_shift,
    )
    mixed_res = (
        signal.astype(jnp.float32)
        + jnp.dot(activated, point_out, preferred_element_type=jnp.float32)
    ).astype(jnp.bfloat16)
    moe_in = layer_norm(mixed_res).astype(jnp.bfloat16)
    route_ids = expert_ids[0, :, 0]
    expert_count = router.shape[1]
    capacity = 2 * frame_count // expert_count
    owners = lax.axis_size("expert")
    per_owner = expert_count // owners
    labels = jnp.arange(expert_count, dtype=jnp.int32)
    onehot = (route_ids[:, None] == labels[None, :]).astype(jnp.int32)
    earlier = jnp.cumsum(onehot, axis=0, dtype=jnp.int32) - onehot
    rank_in = jnp.sum(earlier * onehot, axis=1, dtype=jnp.int32)
    logits = jnp.dot(moe_in, router, preferred_element_type=jnp.float32)
    gate_value = jax.nn.sigmoid(jnp.sum(logits * onehot.astype(jnp.float32), axis=1))
    owner_group = route_ids // per_owner
    member = route_ids % per_owner
    slot_index = (member * owners + owner_group) * capacity + rank_in
    slot_count = per_owner * owners * capacity
    placing = (slot_index[:, None] == jnp.arange(slot_count, dtype=jnp.int32)[None, :]).astype(
        jnp.bfloat16
    )
    send_buffer = lax.dot_general(
        placing, moe_in, (((0,), (0,)), ((), ())), preferred_element_type=jnp.float32
    ).astype(jnp.bfloat16)
    send_buffer = send_buffer.reshape(owners * per_owner, capacity, model_width)
    w_in = expert_in[0, 0]
    w_out = expert_out[0, 0]
    by_member = lax.all_to_all(send_buffer, ("z", "expert"), split_axis=0, concat_axis=0, tiled=True)
    gathered = lax.all_gather(by_member, "y", axis=0, tiled=False)
    partial_out = expert_pass(gathered, w_in, w_out)
    summed = lax.psum_scatter(partial_out, "y", scatter_dimension=0, tiled=False)
    results = lax.all_to_all(summed, ("z", "expert"), split_axis=0, concat_axis=0, tiled=True)
    frame_moe = jnp.dot(
        placing, results.reshape(-1, model_width), preferred_element_type=jnp.float32
    )
    layer_out = mixed_res.astype(jnp.float32) + gate_value[:, None] * frame_moe.astype(jnp.float32)
    return layer_out.astype(jnp.bfloat16)[None]


def solution(mesh):
    tm_size = mesh.shape["tm"]
    y_size = QUARTERS
    split_mesh = Mesh(
        mesh.devices.reshape(tm_size // y_size, y_size, mesh.shape["expert"]), ("z", "y", "expert")
    )
    frames_spec = P("expert", ("z", "y"), None)
    weights_spec = P("expert", ("z", "y"), None, None)
    return jax.shard_map(
        shards,
        mesh=split_mesh,
        in_specs=(
            frames_spec,
            P("expert", None),
            frames_spec,
            P(),
            P(),
            P(),
            P(),
            P(),
            P(),
            weights_spec,
            weights_spec,
        ),
        out_specs=frames_spec,
        check_vma=False,
    )
```

```python
import jax
import jax.numpy as jnp
from jax import lax
from jax.experimental import pallas as pl
from jax.experimental.pallas import tpu as pltpu
from jax.sharding import Mesh, PartitionSpec as P

QUARTERS = 4
ROW_BLOCK = 32
LANE_BLOCK = 512
ROW_TILE = 512


def depthwise_kernel(
    gated_ref,
    before_ref,
    after_ref,
    taps_ref,
    first_ref,
    last_ref,
    scale_ref,
    shift_ref,
    out_ref,
    wide_ref,
    shifted_ref,
):
    frame_count = out_ref.shape[0]
    tap_count = taps_ref.shape[0]
    half_span = (tap_count - 1) // 2
    phases = 8
    span = shifted_ref.shape[1]
    wide_ref[:half_span, :] = before_ref[...].astype(jnp.float32)
    wide_ref[half_span : half_span + frame_count, :] = gated_ref[...].astype(jnp.float32)
    wide_ref[half_span + frame_count :, :] = after_ref[...].astype(jnp.float32)
    for phase in range(phases):
        count = min(span, wide_ref.shape[0] - phase)
        shifted_ref[phase, :count, :] = wide_ref[phase : phase + count, :]
    for row in range(0, frame_count, ROW_BLOCK):
        first_rel = first_ref[row : row + ROW_BLOCK, :]
        last_rel = last_ref[row : row + ROW_BLOCK, :]
        acc = jnp.zeros((ROW_BLOCK, out_ref.shape[1]), jnp.float32)
        for tap in range(tap_count):
            offset = tap - half_span
            phase, base = tap % phases, tap - tap % phases
            window = shifted_ref[phase, row + base : row + base + ROW_BLOCK, :]
            valid = (first_rel <= offset) & (offset < last_rel)
            window = jnp.where(valid, window, 0.0)
            acc = acc + taps_ref[tap : tap + 1, :] * window
        value = acc * scale_ref[...] + shift_ref[...]
        out_ref[row : row + ROW_BLOCK, :] = (value * jax.nn.sigmoid(value)).astype(out_ref.dtype)


def depthwise_silu(gated, before, after, taps, first_rel, last_rel, scale, shift):
    frame_count, width = gated.shape
    tap_count = taps.shape[0]
    half_span = (tap_count - 1) // 2
    rows = frame_count + 2 * half_span
    span = frame_count + 24
    return pl.pallas_call(
        depthwise_kernel,
        grid=(width // LANE_BLOCK,),
        in_specs=[
            pl.BlockSpec((frame_count, LANE_BLOCK), lambda c: (0, c)),
            pl.BlockSpec((half_span, LANE_BLOCK), lambda c: (0, c)),
            pl.BlockSpec((half_span, LANE_BLOCK), lambda c: (0, c)),
            pl.BlockSpec((tap_count, LANE_BLOCK), lambda c: (0, c)),
            pl.BlockSpec((frame_count, 1), lambda c: (0, 0)),
            pl.BlockSpec((frame_count, 1), lambda c: (0, 0)),
            pl.BlockSpec((1, LANE_BLOCK), lambda c: (0, c)),
            pl.BlockSpec((1, LANE_BLOCK), lambda c: (0, c)),
        ],
        out_specs=pl.BlockSpec((frame_count, LANE_BLOCK), lambda c: (0, c)),
        out_shape=jax.ShapeDtypeStruct((frame_count, width), jnp.bfloat16),
        scratch_shapes=[
            pltpu.VMEM((rows, LANE_BLOCK), jnp.float32),
            pltpu.VMEM((8, span, LANE_BLOCK), jnp.float32),
        ],
    )(gated, before, after, taps, first_rel, last_rel, scale.reshape(1, -1), shift.reshape(1, -1))


def halo_pair(cells, axis, width):
    count = lax.axis_size(axis)
    ends = count - 1
    head = cells[:width]
    tail = cells[cells.shape[0] - width :]
    before = lax.ppermute(tail, axis, [(i, (i + 1) % count) for i in range(ends)])
    after = lax.ppermute(head, axis, [((i + 1) % count, i) for i in range(ends)])
    return before, after


def layer_norm(values):
    values = values.astype(jnp.float32)
    center = values - jnp.mean(values, axis=-1, keepdims=True)
    variance = jnp.mean(center * center, axis=-1, keepdims=True)
    return center * lax.rsqrt(variance + 1e-05)


def expert_kernel(rows_ref, w_in_ref, w_out_ref, out_ref):
    hidden = jnp.dot(rows_ref[...], w_in_ref[...], preferred_element_type=jnp.float32)
    hidden = (hidden * jax.nn.sigmoid(hidden)).astype(jnp.bfloat16)
    out_ref[...] = jnp.dot(hidden, w_out_ref[...], preferred_element_type=jnp.float32).astype(
        out_ref.dtype
    )


def expert_pass(slot_block, w_in, w_out):
    slot_rows = slot_block.reshape(-1, slot_block.shape[-1])
    row_count, model_width = slot_rows.shape
    hidden_width = w_in.shape[1]
    tile = min(ROW_TILE, row_count)
    partial_out = pl.pallas_call(
        expert_kernel,
        grid=(row_count // tile,),
        in_specs=[
            pl.BlockSpec((tile, model_width), lambda r: (r, 0)),
            pl.BlockSpec((model_width, hidden_width), lambda r: (0, 0)),
            pl.BlockSpec((hidden_width, model_width), lambda r: (0, 0)),
        ],
        out_specs=pl.BlockSpec((tile, model_width), lambda r: (r, 0)),
        out_shape=jax.ShapeDtypeStruct((row_count, model_width), jnp.bfloat16),
    )(slot_rows, w_in, w_out)
    return partial_out.reshape(slot_block.shape)


def others_kernel(own_ref, rows_ref, own_part_ref, w_in_ref, w_out_ref, out_ref):
    mine = pl.program_id(0) == own_ref[0]

    @pl.when(mine)
    def _():
        out_ref[...] = own_part_ref[...]

    @pl.when(jnp.logical_not(mine))
    def _():
        expert_kernel(rows_ref, w_in_ref, w_out_ref, out_ref)


def expert_pass_others(gathered, own_partial, own_index, w_in, w_out):
    blocks = gathered.shape[0]
    model_width = gathered.shape[-1]
    slot_rows = gathered.reshape(-1, model_width)
    row_count = slot_rows.shape[0]
    tile = row_count // blocks
    hidden_width = w_in.shape[1]
    own_rows = own_partial.reshape(-1, model_width)
    partial_out = pl.pallas_call(
        others_kernel,
        grid_spec=pltpu.PrefetchScalarGridSpec(
            num_scalar_prefetch=1,
            grid=(blocks,),
            in_specs=[
                pl.BlockSpec((tile, model_width), lambda r, own: (r, 0)),
                pl.BlockSpec((tile, model_width), lambda r, own: (0, 0)),
                pl.BlockSpec((model_width, hidden_width), lambda r, own: (0, 0)),
                pl.BlockSpec((hidden_width, model_width), lambda r, own: (0, 0)),
            ],
            out_specs=pl.BlockSpec((tile, model_width), lambda r, own: (r, 0)),
        ),
        out_shape=jax.ShapeDtypeStruct((row_count, model_width), jnp.bfloat16),
    )(own_index, slot_rows, own_rows, w_in, w_out)
    return partial_out.reshape(gathered.shape)


def shards(
    frames,
    utt_lengths,
    expert_ids,
    point_in,
    depth_taps,
    norm_scale,
    norm_shift,
    point_out,
    router,
    expert_in,
    expert_out,
):
    signal = frames[0]
    frame_count, model_width = signal.shape
    tap_count = depth_taps.shape[0]
    half_span = (tap_count - 1) // 2
    normed = layer_norm(signal).astype(jnp.bfloat16)
    projected = jnp.dot(normed, point_in, preferred_element_type=jnp.float32)
    gated_act = (projected[:, :model_width] * jax.nn.sigmoid(projected[:, model_width:])).astype(
        jnp.bfloat16
    )
    before, after = halo_pair(gated_act, ("z", "y"), half_span)
    lengths = utt_lengths[0]
    utter_ends = jnp.cumsum(lengths, dtype=jnp.int32)
    utter_starts = utter_ends - lengths
    position = (lax.axis_index("z") * lax.axis_size("y") + lax.axis_index("y")) * frame_count + jnp.arange(frame_count, dtype=jnp.int32)
    inside = (utter_starts[None, :] <= position[:, None]) & (
        position[:, None] < utter_ends[None, :]
    )
    first_pos = jnp.sum(jnp.where(inside, utter_starts[None, :], 0), axis=1, dtype=jnp.int32)
    last_pos = jnp.sum(jnp.where(inside, utter_ends[None, :], 0), axis=1, dtype=jnp.int32)
    activated = depthwise_silu(
        gated_act,
        before,
        after,
        depth_taps,
        (first_pos - position)[:, None],
        (last_pos - position)[:, None],
        norm_scale,
        norm_shift,
    )
    mixed_res = (
        signal.astype(jnp.float32)
        + jnp.dot(activated, point_out, preferred_element_type=jnp.float32)
    ).astype(jnp.bfloat16)
    moe_in = layer_norm(mixed_res).astype(jnp.bfloat16)
    route_ids = expert_ids[0, :, 0]
    expert_count = router.shape[1]
    capacity = 2 * frame_count // expert_count
    owners = lax.axis_size("expert")
    per_owner = expert_count // owners
    labels = jnp.arange(expert_count, dtype=jnp.int32)
    onehot = (route_ids[:, None] == labels[None, :]).astype(jnp.int32)
    earlier = jnp.cumsum(onehot, axis=0, dtype=jnp.int32) - onehot
    rank_in = jnp.sum(earlier * onehot, axis=1, dtype=jnp.int32)
    logits = jnp.dot(moe_in, router, preferred_element_type=jnp.float32)
    gate_value = jax.nn.sigmoid(jnp.sum(logits * onehot.astype(jnp.float32), axis=1))
    owner_group = route_ids // per_owner
    member = route_ids % per_owner
    slot_index = (member * owners + owner_group) * capacity + rank_in
    slot_count = per_owner * owners * capacity
    placing = (slot_index[:, None] == jnp.arange(slot_count, dtype=jnp.int32)[None, :]).astype(
        jnp.bfloat16
    )
    send_buffer = lax.dot_general(
        placing, moe_in, (((0,), (0,)), ((), ())), preferred_element_type=jnp.float32
    ).astype(jnp.bfloat16)
    send_buffer = send_buffer.reshape(owners * per_owner, capacity, model_width)
    w_in = expert_in[0, 0]
    w_out = expert_out[0, 0]
    by_member = lax.all_to_all(send_buffer, ("z", "expert"), split_axis=0, concat_axis=0, tiled=True)
    own_partial = expert_pass(by_member, w_in, w_out)
    gathered = lax.all_gather(by_member, "y", axis=0, tiled=False)
    own_index = lax.axis_index("y").astype(jnp.int32).reshape(1)
    partial_out = expert_pass_others(gathered, own_partial, own_index, w_in, w_out)
    summed = lax.psum_scatter(partial_out, "y", scatter_dimension=0, tiled=False)
    results = lax.all_to_all(summed, ("z", "expert"), split_axis=0, concat_axis=0, tiled=True)
    frame_moe = jnp.dot(
        placing, results.reshape(-1, model_width), preferred_element_type=jnp.float32
    )
    layer_out = mixed_res.astype(jnp.float32) + gate_value[:, None] * frame_moe.astype(jnp.float32)
    return layer_out.astype(jnp.bfloat16)[None]


def solution(mesh):
    tm_size = mesh.shape["tm"]
    y_size = QUARTERS
    split_mesh = Mesh(
        mesh.devices.reshape(tm_size // y_size, y_size, mesh.shape["expert"]), ("z", "y", "expert")
    )
    frames_spec = P("expert", ("z", "y"), None)
    weights_spec = P("expert", ("z", "y"), None, None)
    return jax.shard_map(
        shards,
        mesh=split_mesh,
        in_specs=(
            frames_spec,
            P("expert", None),
            frames_spec,
            P(),
            P(),
            P(),
            P(),
            P(),
            P(),
            weights_spec,
            weights_spec,
        ),
        out_specs=frames_spec,
        check_vma=False,
    )
```

```python
import jax
import jax.numpy as jnp
from jax import lax
from jax.experimental import pallas as pl
from jax.experimental.pallas import tpu as pltpu
from jax.sharding import Mesh, PartitionSpec as P

QUARTERS = 4
ROW_BLOCK = 32
LANE_BLOCK = 512
ROW_TILE = 1024


def depthwise_kernel(
    gated_ref,
    before_ref,
    after_ref,
    taps_ref,
    first_ref,
    last_ref,
    scale_ref,
    shift_ref,
    out_ref,
    wide_ref,
    shifted_ref,
):
    frame_count = out_ref.shape[0]
    tap_count = taps_ref.shape[0]
    half_span = (tap_count - 1) // 2
    phases = 8
    span = shifted_ref.shape[1]
    wide_ref[:half_span, :] = before_ref[...].astype(jnp.float32)
    wide_ref[half_span : half_span + frame_count, :] = gated_ref[...].astype(jnp.float32)
    wide_ref[half_span + frame_count :, :] = after_ref[...].astype(jnp.float32)
    for phase in range(phases):
        count = min(span, wide_ref.shape[0] - phase)
        shifted_ref[phase, :count, :] = wide_ref[phase : phase + count, :]
    for row in range(0, frame_count, ROW_BLOCK):
        first_rel = first_ref[row : row + ROW_BLOCK, :]
        last_rel = last_ref[row : row + ROW_BLOCK, :]
        acc = jnp.zeros((ROW_BLOCK, out_ref.shape[1]), jnp.float32)
        for tap in range(tap_count):
            offset = tap - half_span
            phase, base = tap % phases, tap - tap % phases
            window = shifted_ref[phase, row + base : row + base + ROW_BLOCK, :]
            valid = (first_rel <= offset) & (offset < last_rel)
            window = jnp.where(valid, window, 0.0)
            acc = acc + taps_ref[tap : tap + 1, :] * window
        value = acc * scale_ref[...] + shift_ref[...]
        out_ref[row : row + ROW_BLOCK, :] = (value * jax.nn.sigmoid(value)).astype(out_ref.dtype)


def depthwise_silu(gated, before, after, taps, first_rel, last_rel, scale, shift):
    frame_count, width = gated.shape
    tap_count = taps.shape[0]
    half_span = (tap_count - 1) // 2
    rows = frame_count + 2 * half_span
    span = frame_count + 24
    return pl.pallas_call(
        depthwise_kernel,
        grid=(width // LANE_BLOCK,),
        in_specs=[
            pl.BlockSpec((frame_count, LANE_BLOCK), lambda c: (0, c)),
            pl.BlockSpec((half_span, LANE_BLOCK), lambda c: (0, c)),
            pl.BlockSpec((half_span, LANE_BLOCK), lambda c: (0, c)),
            pl.BlockSpec((tap_count, LANE_BLOCK), lambda c: (0, c)),
            pl.BlockSpec((frame_count, 1), lambda c: (0, 0)),
            pl.BlockSpec((frame_count, 1), lambda c: (0, 0)),
            pl.BlockSpec((1, LANE_BLOCK), lambda c: (0, c)),
            pl.BlockSpec((1, LANE_BLOCK), lambda c: (0, c)),
        ],
        out_specs=pl.BlockSpec((frame_count, LANE_BLOCK), lambda c: (0, c)),
        out_shape=jax.ShapeDtypeStruct((frame_count, width), jnp.bfloat16),
        scratch_shapes=[
            pltpu.VMEM((rows, LANE_BLOCK), jnp.float32),
            pltpu.VMEM((8, span, LANE_BLOCK), jnp.float32),
        ],
    )(gated, before, after, taps, first_rel, last_rel, scale.reshape(1, -1), shift.reshape(1, -1))


def halo_pair(cells, axis, width):
    count = lax.axis_size(axis)
    ends = count - 1
    head = cells[:width]
    tail = cells[cells.shape[0] - width :]
    before = lax.ppermute(tail, axis, [(i, (i + 1) % count) for i in range(ends)])
    after = lax.ppermute(head, axis, [((i + 1) % count, i) for i in range(ends)])
    return before, after


def layer_norm(values):
    values = values.astype(jnp.float32)
    center = values - jnp.mean(values, axis=-1, keepdims=True)
    variance = jnp.mean(center * center, axis=-1, keepdims=True)
    return center * lax.rsqrt(variance + 1e-05)


def expert_kernel(rows_ref, w_in_ref, w_out_ref, out_ref):
    hidden = jnp.dot(rows_ref[...], w_in_ref[...], preferred_element_type=jnp.float32)
    hidden = (hidden * jax.nn.sigmoid(hidden)).astype(jnp.bfloat16)
    out_ref[...] = jnp.dot(hidden, w_out_ref[...], preferred_element_type=jnp.float32).astype(
        out_ref.dtype
    )


def expert_pass(slot_block, w_in, w_out):
    slot_rows = slot_block.reshape(-1, slot_block.shape[-1])
    row_count, model_width = slot_rows.shape
    hidden_width = w_in.shape[1]
    tile = min(ROW_TILE, row_count)
    partial_out = pl.pallas_call(
        expert_kernel,
        grid=(row_count // tile,),
        in_specs=[
            pl.BlockSpec((tile, model_width), lambda r: (r, 0)),
            pl.BlockSpec((model_width, hidden_width), lambda r: (0, 0)),
            pl.BlockSpec((hidden_width, model_width), lambda r: (0, 0)),
        ],
        out_specs=pl.BlockSpec((tile, model_width), lambda r: (r, 0)),
        out_shape=jax.ShapeDtypeStruct((row_count, model_width), jnp.bfloat16),
    )(slot_rows, w_in, w_out)
    return partial_out.reshape(slot_block.shape)


def shards(
    frames,
    utt_lengths,
    expert_ids,
    point_in,
    depth_taps,
    norm_scale,
    norm_shift,
    point_out,
    router,
    expert_in,
    expert_out,
):
    signal = frames[0]
    frame_count, model_width = signal.shape
    tap_count = depth_taps.shape[0]
    half_span = (tap_count - 1) // 2
    normed = layer_norm(signal).astype(jnp.bfloat16)
    projected = jnp.dot(normed, point_in, preferred_element_type=jnp.float32)
    gated_act = (projected[:, :model_width] * jax.nn.sigmoid(projected[:, model_width:])).astype(
        jnp.bfloat16
    )
    before, after = halo_pair(gated_act, ("z", "y"), half_span)
    lengths = utt_lengths[0]
    utter_ends = jnp.cumsum(lengths, dtype=jnp.int32)
    utter_starts = utter_ends - lengths
    position = (lax.axis_index("z") * lax.axis_size("y") + lax.axis_index("y")) * frame_count + jnp.arange(frame_count, dtype=jnp.int32)
    inside = (utter_starts[None, :] <= position[:, None]) & (
        position[:, None] < utter_ends[None, :]
    )
    first_pos = jnp.sum(jnp.where(inside, utter_starts[None, :], 0), axis=1, dtype=jnp.int32)
    last_pos = jnp.sum(jnp.where(inside, utter_ends[None, :], 0), axis=1, dtype=jnp.int32)
    activated = depthwise_silu(
        gated_act,
        before,
        after,
        depth_taps,
        (first_pos - position)[:, None],
        (last_pos - position)[:, None],
        norm_scale,
        norm_shift,
    )
    mixed_res = (
        signal.astype(jnp.float32)
        + jnp.dot(activated, point_out, preferred_element_type=jnp.float32)
    ).astype(jnp.bfloat16)
    moe_in = layer_norm(mixed_res).astype(jnp.bfloat16)
    route_ids = expert_ids[0, :, 0]
    expert_count = router.shape[1]
    capacity = 2 * frame_count // expert_count
    owners = lax.axis_size("expert")
    per_owner = expert_count // owners
    labels = jnp.arange(expert_count, dtype=jnp.int32)
    onehot = (route_ids[:, None] == labels[None, :]).astype(jnp.int32)
    earlier = jnp.cumsum(onehot, axis=0, dtype=jnp.int32) - onehot
    rank_in = jnp.sum(earlier * onehot, axis=1, dtype=jnp.int32)
    logits = jnp.dot(moe_in, router, preferred_element_type=jnp.float32)
    gate_value = jax.nn.sigmoid(jnp.sum(logits * onehot.astype(jnp.float32), axis=1))
    owner_group = route_ids // per_owner
    member = route_ids % per_owner
    slot_index = (member * owners + owner_group) * capacity + rank_in
    slot_count = per_owner * owners * capacity
    placing = (slot_index[:, None] == jnp.arange(slot_count, dtype=jnp.int32)[None, :]).astype(
        jnp.bfloat16
    )
    send_buffer = lax.dot_general(
        placing, moe_in, (((0,), (0,)), ((), ())), preferred_element_type=jnp.float32
    ).astype(jnp.bfloat16)
    send_buffer = send_buffer.reshape(owners * per_owner, capacity, model_width)
    w_in = expert_in[0, 0]
    w_out = expert_out[0, 0]
    by_member = lax.all_to_all(send_buffer, ("z", "expert"), split_axis=0, concat_axis=0, tiled=True)
    gathered = lax.all_gather(by_member, "y", axis=0, tiled=False)
    partial_out = expert_pass(gathered, w_in, w_out)
    summed = lax.psum_scatter(partial_out, "y", scatter_dimension=0, tiled=False)
    results = lax.all_to_all(summed, ("z", "expert"), split_axis=0, concat_axis=0, tiled=True)
    frame_moe = jnp.dot(
        placing, results.reshape(-1, model_width), preferred_element_type=jnp.float32
    )
    layer_out = mixed_res.astype(jnp.float32) + gate_value[:, None] * frame_moe.astype(jnp.float32)
    return layer_out.astype(jnp.bfloat16)[None]


def solution(mesh):
    tm_size = mesh.shape["tm"]
    y_size = QUARTERS
    split_mesh = Mesh(
        mesh.devices.reshape(tm_size // y_size, y_size, mesh.shape["expert"]), ("z", "y", "expert")
    )
    frames_spec = P("expert", ("z", "y"), None)
    weights_spec = P("expert", ("z", "y"), None, None)
    return jax.shard_map(
        shards,
        mesh=split_mesh,
        in_specs=(
            frames_spec,
            P("expert", None),
            frames_spec,
            P(),
            P(),
            P(),
            P(),
            P(),
            P(),
            weights_spec,
            weights_spec,
        ),
        out_specs=frames_spec,
        check_vma=False,
    )
```

```python
import jax
import jax.numpy as jnp
from jax import lax
from jax.experimental import pallas as pl
from jax.experimental.pallas import tpu as pltpu
from jax.sharding import Mesh, PartitionSpec as P

QUARTERS = 4
ROW_BLOCK = 16
LANE_BLOCK = 1024
ROW_TILE = 512


def depthwise_kernel(
    gated_ref,
    before_ref,
    after_ref,
    taps_ref,
    first_ref,
    last_ref,
    scale_ref,
    shift_ref,
    out_ref,
    wide_ref,
    shifted_ref,
):
    frame_count = out_ref.shape[0]
    tap_count = taps_ref.shape[0]
    half_span = (tap_count - 1) // 2
    phases = 8
    span = shifted_ref.shape[1]
    wide_ref[:half_span, :] = before_ref[...].astype(jnp.float32)
    wide_ref[half_span : half_span + frame_count, :] = gated_ref[...].astype(jnp.float32)
    wide_ref[half_span + frame_count :, :] = after_ref[...].astype(jnp.float32)
    for phase in range(phases):
        count = min(span, wide_ref.shape[0] - phase)
        shifted_ref[phase, :count, :] = wide_ref[phase : phase + count, :]
    for row in range(0, frame_count, ROW_BLOCK):
        first_rel = first_ref[row : row + ROW_BLOCK, :]
        last_rel = last_ref[row : row + ROW_BLOCK, :]
        acc = jnp.zeros((ROW_BLOCK, out_ref.shape[1]), jnp.float32)
        for tap in range(tap_count):
            offset = tap - half_span
            phase, base = tap % phases, tap - tap % phases
            window = shifted_ref[phase, row + base : row + base + ROW_BLOCK, :]
            valid = (first_rel <= offset) & (offset < last_rel)
            window = jnp.where(valid, window, 0.0)
            acc = acc + taps_ref[tap : tap + 1, :] * window
        value = acc * scale_ref[...] + shift_ref[...]
        out_ref[row : row + ROW_BLOCK, :] = (value * jax.nn.sigmoid(value)).astype(out_ref.dtype)


def depthwise_silu(gated, before, after, taps, first_rel, last_rel, scale, shift):
    frame_count, width = gated.shape
    tap_count = taps.shape[0]
    half_span = (tap_count - 1) // 2
    rows = frame_count + 2 * half_span
    span = frame_count + 24
    return pl.pallas_call(
        depthwise_kernel,
        grid=(width // LANE_BLOCK,),
        in_specs=[
            pl.BlockSpec((frame_count, LANE_BLOCK), lambda c: (0, c)),
            pl.BlockSpec((half_span, LANE_BLOCK), lambda c: (0, c)),
            pl.BlockSpec((half_span, LANE_BLOCK), lambda c: (0, c)),
            pl.BlockSpec((tap_count, LANE_BLOCK), lambda c: (0, c)),
            pl.BlockSpec((frame_count, 1), lambda c: (0, 0)),
            pl.BlockSpec((frame_count, 1), lambda c: (0, 0)),
            pl.BlockSpec((1, LANE_BLOCK), lambda c: (0, c)),
            pl.BlockSpec((1, LANE_BLOCK), lambda c: (0, c)),
        ],
        out_specs=pl.BlockSpec((frame_count, LANE_BLOCK), lambda c: (0, c)),
        out_shape=jax.ShapeDtypeStruct((frame_count, width), jnp.bfloat16),
        scratch_shapes=[
            pltpu.VMEM((rows, LANE_BLOCK), jnp.float32),
            pltpu.VMEM((8, span, LANE_BLOCK), jnp.float32),
        ],
    )(gated, before, after, taps, first_rel, last_rel, scale.reshape(1, -1), shift.reshape(1, -1))


def halo_pair(cells, axis, width):
    count = lax.axis_size(axis)
    ends = count - 1
    head = cells[:width]
    tail = cells[cells.shape[0] - width :]
    before = lax.ppermute(tail, axis, [(i, (i + 1) % count) for i in range(ends)])
    after = lax.ppermute(head, axis, [((i + 1) % count, i) for i in range(ends)])
    return before, after


def layer_norm(values):
    values = values.astype(jnp.float32)
    center = values - jnp.mean(values, axis=-1, keepdims=True)
    variance = jnp.mean(center * center, axis=-1, keepdims=True)
    return center * lax.rsqrt(variance + 1e-05)


def expert_kernel(rows_ref, w_in_ref, w_out_ref, out_ref):
    hidden = jnp.dot(rows_ref[...], w_in_ref[...], preferred_element_type=jnp.float32)
    hidden = (hidden * jax.nn.sigmoid(hidden)).astype(jnp.bfloat16)
    out_ref[...] = jnp.dot(hidden, w_out_ref[...], preferred_element_type=jnp.float32).astype(
        out_ref.dtype
    )


def expert_pass(slot_block, w_in, w_out):
    slot_rows = slot_block.reshape(-1, slot_block.shape[-1])
    row_count, model_width = slot_rows.shape
    hidden_width = w_in.shape[1]
    tile = min(ROW_TILE, row_count)
    partial_out = pl.pallas_call(
        expert_kernel,
        grid=(row_count // tile,),
        in_specs=[
            pl.BlockSpec((tile, model_width), lambda r: (r, 0)),
            pl.BlockSpec((model_width, hidden_width), lambda r: (0, 0)),
            pl.BlockSpec((hidden_width, model_width), lambda r: (0, 0)),
        ],
        out_specs=pl.BlockSpec((tile, model_width), lambda r: (r, 0)),
        out_shape=jax.ShapeDtypeStruct((row_count, model_width), jnp.bfloat16),
    )(slot_rows, w_in, w_out)
    return partial_out.reshape(slot_block.shape)


def shards(
    frames,
    utt_lengths,
    expert_ids,
    point_in,
    depth_taps,
    norm_scale,
    norm_shift,
    point_out,
    router,
    expert_in,
    expert_out,
):
    signal = frames[0]
    frame_count, model_width = signal.shape
    tap_count = depth_taps.shape[0]
    half_span = (tap_count - 1) // 2
    normed = layer_norm(signal).astype(jnp.bfloat16)
    projected = jnp.dot(normed, point_in, preferred_element_type=jnp.float32)
    gated_act = (projected[:, :model_width] * jax.nn.sigmoid(projected[:, model_width:])).astype(
        jnp.bfloat16
    )
    before, after = halo_pair(gated_act, ("z", "y"), half_span)
    lengths = utt_lengths[0]
    utter_ends = jnp.cumsum(lengths, dtype=jnp.int32)
    utter_starts = utter_ends - lengths
    position = (lax.axis_index("z") * lax.axis_size("y") + lax.axis_index("y")) * frame_count + jnp.arange(frame_count, dtype=jnp.int32)
    inside = (utter_starts[None, :] <= position[:, None]) & (
        position[:, None] < utter_ends[None, :]
    )
    first_pos = jnp.sum(jnp.where(inside, utter_starts[None, :], 0), axis=1, dtype=jnp.int32)
    last_pos = jnp.sum(jnp.where(inside, utter_ends[None, :], 0), axis=1, dtype=jnp.int32)
    activated = depthwise_silu(
        gated_act,
        before,
        after,
        depth_taps,
        (first_pos - position)[:, None],
        (last_pos - position)[:, None],
        norm_scale,
        norm_shift,
    )
    mixed_res = (
        signal.astype(jnp.float32)
        + jnp.dot(activated, point_out, preferred_element_type=jnp.float32)
    ).astype(jnp.bfloat16)
    moe_in = layer_norm(mixed_res).astype(jnp.bfloat16)
    route_ids = expert_ids[0, :, 0]
    expert_count = router.shape[1]
    capacity = 2 * frame_count // expert_count
    owners = lax.axis_size("expert")
    per_owner = expert_count // owners
    labels = jnp.arange(expert_count, dtype=jnp.int32)
    onehot = (route_ids[:, None] == labels[None, :]).astype(jnp.int32)
    earlier = jnp.cumsum(onehot, axis=0, dtype=jnp.int32) - onehot
    rank_in = jnp.sum(earlier * onehot, axis=1, dtype=jnp.int32)
    logits = jnp.dot(moe_in, router, preferred_element_type=jnp.float32)
    gate_value = jax.nn.sigmoid(jnp.sum(logits * onehot.astype(jnp.float32), axis=1))
    owner_group = route_ids // per_owner
    member = route_ids % per_owner
    slot_index = (member * owners + owner_group) * capacity + rank_in
    slot_count = per_owner * owners * capacity
    placing = (slot_index[:, None] == jnp.arange(slot_count, dtype=jnp.int32)[None, :]).astype(
        jnp.bfloat16
    )
    send_buffer = lax.dot_general(
        placing, moe_in, (((0,), (0,)), ((), ())), preferred_element_type=jnp.float32
    ).astype(jnp.bfloat16)
    send_buffer = send_buffer.reshape(owners * per_owner, capacity, model_width)
    w_in = expert_in[0, 0]
    w_out = expert_out[0, 0]
    by_member = lax.all_to_all(send_buffer, ("z", "expert"), split_axis=0, concat_axis=0, tiled=True)
    gathered = lax.all_gather(by_member, "y", axis=0, tiled=False)
    partial_out = expert_pass(gathered, w_in, w_out)
    summed = lax.psum_scatter(partial_out, "y", scatter_dimension=0, tiled=False)
    results = lax.all_to_all(summed, ("z", "expert"), split_axis=0, concat_axis=0, tiled=True)
    frame_moe = jnp.dot(
        placing, results.reshape(-1, model_width), preferred_element_type=jnp.float32
    )
    layer_out = mixed_res.astype(jnp.float32) + gate_value[:, None] * frame_moe.astype(jnp.float32)
    return layer_out.astype(jnp.bfloat16)[None]


def solution(mesh):
    tm_size = mesh.shape["tm"]
    y_size = QUARTERS
    split_mesh = Mesh(
        mesh.devices.reshape(tm_size // y_size, y_size, mesh.shape["expert"]), ("z", "y", "expert")
    )
    frames_spec = P("expert", ("z", "y"), None)
    weights_spec = P("expert", ("z", "y"), None, None)
    return jax.shard_map(
        shards,
        mesh=split_mesh,
        in_specs=(
            frames_spec,
            P("expert", None),
            frames_spec,
            P(),
            P(),
            P(),
            P(),
            P(),
            P(),
            weights_spec,
            weights_spec,
        ),
        out_specs=frames_spec,
        check_vma=False,
    )
```
